32 devices in a mesh: tm: 4 (over z), space: 2 (over y), hyp: 4 (over x, core).
Axes of the slice: x: 2, y: 2, z: 4, core: 2. Of those that a mesh axis runs over, the one named last changes fastest.
Arguments:
- log_kappa: float32 [8192], P('space'), may hold values from -0.5 to 0.5
- node_mass: float32 [8192], P('space'), may hold values from 0.5 to 2
- rho_base: float32 [8192], P('space'), may hold values from 1.5 to 4
- edge_weight: float32 [4, 8192], P(None, 'space'), may hold values from 0.05 to 0.3
- offsets: int32 [4, 8192], P(None, 'space'), may hold values from -64 to 64
- roughness: float32 [64, 8192], P('tm', 'space'), may hold values from 0.5 to 1.0002
- coupling: float32 [64, 8192], P('tm', 'space'), may hold values from 0.5 to 1
- obs_weight: float32 [64, 8192], P('tm', 'space'), may hold values from 0.0003 to 0.03
- observed: float32 [64, 8192], P('tm', 'space'), may hold values from -0.3125 to 0.3125
- hyper_params: float32 [4], replicated, may hold values from -0.3 to 0.3
Outputs:
- solution: float32 [64, 8192], P('tm', ('space', 'hyp'))
- log_det_mean: float32 [8192], P('space')
- gradient: float32 [4, 8192], P(None, 'space')
The draws below stay inside these ranges and needn't reach their ends.
Inputs may be any that keep to these rules, and one draw needn't show every extreme that they name: offsets[k, i] is a band offset from node i to a listed neighbour.
All inputs are finite; a program needn't handle non-finite values.
Results may differ from the reference program's by a relative error of at most 0.0003.
Values sent between devices are 32-bit elements; how exact they have to be, the bound alone decides.
No kernel may reach another device: no remote copies, remote signals or barrier semaphores. Data moves between devices by JAX's collectives and lax.ppermute only.
A program may use at most 64 MiB of HBM per device.

```python
import math
import jax
import jax.numpy as jnp
from jax import lax

BAND = 64
NEIGH = 4
NDIR = 4
NODES = 8192
BLOCKS = 64


def coupling_law(key):
    uniform_part = jax.random.uniform(jax.random.fold_in(key, 11), (BLOCKS, NODES), jnp.float32)
    values = 0.5 * jnp.exp(jnp.log(2.0) * uniform_part)
    return values


def draw_coupling(key, part):
    return coupling_law(key)


def draw_roughness(key, part):
    values = coupling_law(key)
    following = jnp.roll(values, -1, axis=0)
    spread = 1.0 + 0.0002 * jax.random.uniform(jax.random.fold_in(key, 12), (BLOCKS, NODES), jnp.float32)
    return 0.5 * (values + following) * spread


def with_ends(entries, own_key, smallest, top_value):
    dims = entries.shape
    index_at = [jax.random.randint(jax.random.fold_in(own_key, axis), (), 0, dims[axis]) for axis in range(len(dims))]
    entries = entries.at[tuple(index_at)].set(smallest)
    longest = dims.index(max(dims))
    index_at[longest] = (index_at[longest] + 1) % dims[longest]
    return entries.at[tuple(index_at)].set(top_value)


def shard_levels(key, extent, cuts, smallest, high):
    loudness, own = 1.0, jax.random.fold_in(key, 6)
    for axis_at, shards_of in cuts:
        draws = jnp.exp(jax.random.uniform(jax.random.fold_in(own, axis_at), (shards_of,), jnp.float32, smallest / len(cuts), high / len(cuts)))
        loudness = loudness * jnp.repeat(draws, extent[axis_at] // shards_of).reshape([-1 if axis == axis_at else 1 for axis in range(len(extent))])
    return loudness


def bell_draw(rng, extent, scale, limit, split=(), kind=jnp.bfloat16):
    values = jax.random.normal(rng, extent, jnp.float32) * scale
    if len(split) > 0:
        values = shard_levels(rng, extent, split, -0.22, 0.18) * values
    return jnp.clip(values, min=-limit, max=limit).astype(kind)


def setup_inputs(seed: int = 0) -> dict:
    key_of = jax.random.split(jax.random.key(seed), 11)
    return {
        "log_kappa": jnp.clip(jax.random.uniform(key_of[0], (NODES,), jnp.float32, -0.5, 0.5) * shard_levels(key_of[0], (NODES,), ((0, 2),), -0.4, 0.0), -0.5, 0.5),
        "node_mass": jnp.clip(jnp.exp(math.log(2.0) - 1.3862944 * jax.random.uniform(key_of[1], (NODES,), jnp.float32) ** shard_levels(key_of[1], (NODES,), ((0, 2),), -0.2, 0.2)), 0.5, 2.0),
        "rho_base": jnp.clip(1.5 + 2.5 * jax.random.uniform(key_of[2], (NODES,), jnp.float32) ** shard_levels(key_of[2], (NODES,), ((0, 2),), -0.2, 0.2), 1.5, 4.0),
        "edge_weight": jnp.clip(jnp.exp(math.log(0.3) - 1.7917595 * jax.random.uniform(key_of[3], (NEIGH, NODES), jnp.float32) ** shard_levels(key_of[3], (NEIGH, NODES), ((1, 2),), -0.2, 0.2)), 0.05, 0.3),
        "offsets": with_ends(jax.random.randint(key_of[4], (NEIGH, NODES), -BAND, BAND + 1), jax.random.fold_in(key_of[4], 1), -BAND, BAND).astype(jnp.int32),
        "roughness": draw_roughness(jax.random.fold_in(key_of[10], 71), 0),
        "coupling": draw_coupling(jax.random.fold_in(key_of[10], 71), 0),
        "obs_weight": jnp.clip(jnp.exp(math.log(0.03) - 4.6051701 * jax.random.uniform(key_of[7], (BLOCKS, NODES), jnp.float32) ** shard_levels(key_of[7], (BLOCKS, NODES), ((0, 4), (1, 2)), -0.2, 0.2)), 0.0003, 0.03),
        "observed": bell_draw(key_of[8], (BLOCKS, NODES), 0.02, 0.3125, ((0, 4), (1, 2)), jnp.float32),
        "hyper_params": jnp.clip(jax.random.uniform(key_of[9], (NDIR,), jnp.float32, -0.3, 0.3), -0.3, 0.3),
    }


def row_terms(scaled, persist, roughness, coupling, obs_weight, nugget_scale, later_rows):
    prior = scaled * (1.0 + persist * persist) * roughness
    nugget = nugget_scale * obs_weight
    diagonal = prior + nugget
    offdiag = -persist * scaled * coupling * later_rows
    slopes = jnp.stack([2.0 * prior, prior, 2.0 * persist * (1.0 - persist * persist) * scaled * roughness, nugget], axis=-2)
    return diagonal, offdiag, slopes


def reference(log_kappa, node_mass, rho_base, edge_weight, offsets, roughness, coupling, obs_weight, observed, hyper_params):
    node_count = log_kappa.shape[0]
    block_count = roughness.shape[0]
    kappa_sq = jnp.exp(2.0 * log_kappa)
    margin = jnp.zeros((BAND,), kappa_sq.dtype)
    padded = jnp.concatenate([margin, kappa_sq, margin])
    indices = jnp.arange(node_count, dtype=jnp.int32)[None, :] + BAND + offsets
    nearby = jnp.take(padded, indices)
    spatial = jnp.exp(2.0 * hyper_params[0]) * (node_mass * kappa_sq + jnp.sum(edge_weight * nearby, axis=0))
    scaled = jnp.exp(hyper_params[1]) * spatial
    persist = jnp.tanh(hyper_params[2] + rho_base)
    nugget_scale = jnp.exp(hyper_params[3])
    log_slope = jnp.stack([2.0 * jnp.ones_like(persist), jnp.ones_like(persist), (1.0 - persist * persist) / persist, jnp.zeros_like(persist)])
    later_all = (jnp.arange(block_count) > 0).astype(scaled.dtype)
    zeros_row = jnp.zeros_like(persist)
    zeros_dir = jnp.zeros_like(log_slope)

    def forward(carried, step_rows):
        inverse, tangent, solved, scores, log_total = carried
        rough_row, coupling_row, weight_row, observed_row, later_row = step_rows
        diagonal, offdiag, slopes = row_terms(scaled, persist, rough_row, coupling_row, weight_row, nugget_scale, later_row)
        pivots = diagonal - offdiag * offdiag * inverse
        ratios = offdiag * inverse
        tangent = ratios * ratios * tangent + slopes - 2.0 * log_slope * offdiag * ratios
        solved = observed_row - ratios * solved
        scores = scores + 0.5 * tangent / pivots
        log_total = log_total + jnp.log(pivots)
        return (1.0 / pivots, tangent, solved, scores, log_total), (pivots, solved)

    start = (zeros_row, zeros_dir, zeros_row, zeros_dir, zeros_row)
    ending, stacked = lax.scan(forward, start, (roughness, coupling, obs_weight, observed, later_all))
    pivot_rows, solved_rows = stacked
    scores = ending[3]
    log_total = ending[4]

    def backward(carried, step_rows):
        following, quadratic = carried
        rough_row, coupling_row, weight_row, later_row, pivots, solved = step_rows
        diagonal, offdiag, slopes = row_terms(scaled, persist, rough_row, coupling_row, weight_row, nugget_scale, later_row)
        values = (solved - following) / pivots
        quadratic = quadratic + slopes * values * values + 2.0 * log_slope * values * following
        return (offdiag * values, quadratic), values

    closing, solution = lax.scan(backward, (zeros_row, zeros_dir), (roughness, coupling, obs_weight, later_all, pivot_rows, solved_rows), reverse=True)
    quadratic = closing[1]
    log_det_mean = log_total / block_count
    gradient = (scores - 0.5 * quadratic) / block_count
    return solution, log_det_mean, gradient
```

```python
import jax
import jax.numpy as jnp
from jax import lax
from jax.experimental import pallas as pl
from jax.experimental.pallas import tpu as pltpu
from jax.sharding import PartitionSpec as P

BAND = 64
INTERPRET = False


def with_halo(block, sides, width):
    for axis, dim in sides:
        count = lax.axis_size(axis)
        forward = [(i, i + 1) for i in range(count - 1)]
        backward = [(target, source) for source, target in forward]
        low = lax.ppermute(
            lax.slice_in_dim(block, block.shape[dim] - width, None, axis=dim), axis, forward
        )
        high = lax.ppermute(lax.slice_in_dim(block, 0, width, axis=dim), axis, backward)
        block = jnp.concatenate([low, block, high], axis=dim)
    return block


def chain_kernel(data_ref, par_ref, sol_ref, stat_ref, piv_ref, slv_ref):
    rows = data_ref.shape[1]
    ns = par_ref[2:3, :]
    ls2 = par_ref[3:4, :]
    sp = par_ref[4:5, :]
    mps = par_ref[5:6, :]
    qs = par_ref[6:7, :]
    two_ls2 = 2.0 * ls2
    zeros = jnp.zeros_like(sp)

    def forward(t, carry):
        inv, t0, t1, t2, t3, solved, c0, c1, c2, c3, logs = carry
        rough = data_ref[0, pl.ds(t, 1), :]
        coup = data_ref[1, pl.ds(t, 1), :]
        weight = data_ref[2, pl.ds(t, 1), :]
        obs = data_ref[3, pl.ds(t, 1), :]
        prior = sp * rough
        nugget = ns * weight
        diagonal = prior + nugget
        offdiag = mps * coup
        pivots = diagonal - offdiag * offdiag * inv
        ratios = offdiag * inv
        rr = ratios * ratios
        t0 = rr * t0 + 2.0 * prior - 4.0 * offdiag * ratios
        t1 = rr * t1 + prior - 2.0 * offdiag * ratios
        t2 = rr * t2 + qs * rough - two_ls2 * offdiag * ratios
        t3 = rr * t3 + nugget
        solved = obs - ratios * solved
        c0 = c0 + 0.5 * t0 / pivots
        c1 = c1 + 0.5 * t1 / pivots
        c2 = c2 + 0.5 * t2 / pivots
        c3 = c3 + 0.5 * t3 / pivots
        logs = logs + jnp.log(pivots)
        piv_ref[pl.ds(t, 1), :] = pivots
        slv_ref[pl.ds(t, 1), :] = solved
        return (1.0 / pivots, t0, t1, t2, t3, solved, c0, c1, c2, c3, logs)

    start = (zeros,) * 11
    ending = lax.fori_loop(0, rows, forward, start, unroll=8)
    c0, c1, c2, c3, logs = ending[6:]

    def backward(i, carry):
        t = rows - 1 - i
        following, q0, q1, q2, q3 = carry
        rough = data_ref[0, pl.ds(t, 1), :]
        coup = data_ref[1, pl.ds(t, 1), :]
        weight = data_ref[2, pl.ds(t, 1), :]
        prior = sp * rough
        nugget = ns * weight
        offdiag = mps * coup
        values = (slv_ref[pl.ds(t, 1), :] - following) / piv_ref[pl.ds(t, 1), :]
        q0 = q0 + 2.0 * prior * values * values + 4.0 * values * following
        q1 = q1 + prior * values * values + 2.0 * values * following
        q2 = q2 + qs * rough * values * values + two_ls2 * values * following
        q3 = q3 + nugget * values * values
        sol_ref[pl.ds(t, 1), :] = values
        return (offdiag * values, q0, q1, q2, q3)

    closing = lax.fori_loop(0, rows, backward, (zeros,) * 5, unroll=8)
    q0, q1, q2, q3 = closing[1:]
    scale = 1.0 / rows
    stat_ref[0:1, :] = logs * scale
    stat_ref[1:2, :] = (c0 - 0.5 * q0) * scale
    stat_ref[2:3, :] = (c1 - 0.5 * q1) * scale
    stat_ref[3:4, :] = (c2 - 0.5 * q2) * scale
    stat_ref[4:5, :] = (c3 - 0.5 * q3) * scale
    stat_ref[5:8, :] = jnp.zeros((3, sp.shape[1]), jnp.float32)


def run_chain(data, params):
    _, rows, width = data.shape
    vmem = pl.BlockSpec(memory_space=pltpu.VMEM)
    return pl.pallas_call(
        chain_kernel,
        out_shape=(
            jax.ShapeDtypeStruct((rows, width), jnp.float32),
            jax.ShapeDtypeStruct((8, width), jnp.float32),
        ),
        in_specs=[vmem, vmem],
        out_specs=(vmem, vmem),
        scratch_shapes=[pltpu.VMEM((rows, width), jnp.float32)] * 2,
        interpret=INTERPRET,
    )(data, params)


def per_device(
    log_kappa,
    node_mass,
    rho_base,
    edge_weight,
    offsets,
    roughness,
    coupling,
    obs_weight,
    observed,
    hyper_params,
):
    row_count, full_width = roughness.shape
    time_count = lax.axis_size("tm")
    hyp_count = lax.axis_size("hyp")
    time_place = lax.axis_index("tm")
    hyp_place = lax.axis_index("hyp")
    quarter = full_width // hyp_count
    chunk = quarter // time_count
    first = hyp_place * quarter + time_place * chunk

    stacked = jnp.stack([roughness, coupling, obs_weight, observed])
    mine = lax.dynamic_slice_in_dim(stacked, hyp_place * quarter, quarter, axis=2)
    data = lax.all_to_all(mine, "tm", 2, 1, tiled=True)

    kappa_sq = jnp.exp(2.0 * log_kappa)
    padded = with_halo(kappa_sq, (("space", 0),), BAND)
    window = lax.dynamic_slice_in_dim(padded, first, chunk + 2 * BAND)
    near_off = lax.dynamic_slice_in_dim(offsets, first, chunk, axis=1)
    weights = lax.dynamic_slice_in_dim(edge_weight, first, chunk, axis=1)
    mass = lax.dynamic_slice_in_dim(node_mass, first, chunk)
    base = lax.dynamic_slice_in_dim(rho_base, first, chunk)
    own_kappa = window[BAND : BAND + chunk]
    nearby = jnp.zeros(near_off.shape, jnp.float32)
    for shift in range(-BAND, BAND + 1):
        nearby = jnp.where(
            near_off == shift, window[None, BAND + shift : BAND + shift + chunk], nearby
        )
    spatial = jnp.exp(2.0 * hyper_params[0]) * (
        mass * own_kappa + jnp.sum(weights * nearby, axis=0)
    )
    scaled = jnp.exp(hyper_params[1]) * spatial
    persist = jnp.tanh(hyper_params[2] + base)
    nugget_scale = jnp.exp(hyper_params[3]) + jnp.zeros_like(persist)
    log_slope = (1.0 - persist * persist) / persist
    params = jnp.stack(
        [
            scaled,
            persist,
            nugget_scale,
            log_slope,
            scaled * (1.0 + persist * persist),
            -persist * scaled,
            2.0 * persist * (1.0 - persist * persist) * scaled,
            jnp.zeros_like(persist),
        ]
    )
    solution_rows, stats = run_chain(data, params)

    parts = solution_rows.reshape(time_count, row_count, chunk)
    payload = jnp.concatenate(
        [parts, jnp.broadcast_to(stats[None], (time_count,) + stats.shape)], axis=1
    )
    received = lax.all_to_all(payload, "tm", 0, 2, tiled=True)[0]
    solution_out = received[:row_count]
    stats_quarter = received[row_count : row_count + 5]
    stats_full = lax.all_gather(stats_quarter, "hyp", axis=1, tiled=True)
    return (solution_out, stats_full[0], stats_full[1:5])


def solution(mesh):
    placed = (
        P("space"),
        P("space"),
        P("space"),
        P(None, "space"),
        P(None, "space"),
        P("tm", "space"),
        P("tm", "space"),
        P("tm", "space"),
        P("tm", "space"),
        P(),
    )
    return jax.shard_map(
        per_device,
        mesh=mesh,
        in_specs=placed,
        out_specs=(P("tm", ("space", "hyp")), P("space"), P(None, "space")),
        check_vma=False,
    )
```

```python
import jax
import jax.numpy as jnp
from jax import lax
from jax.experimental import pallas as pl
from jax.experimental.pallas import tpu as pltpu
from jax.sharding import PartitionSpec as P

BAND = 64
INTERPRET = False


def with_halo(block, sides, width):
    for axis, dim in sides:
        count = lax.axis_size(axis)
        forward = [(i, i + 1) for i in range(count - 1)]
        backward = [(target, source) for source, target in forward]
        low = lax.ppermute(
            lax.slice_in_dim(block, block.shape[dim] - width, None, axis=dim), axis, forward
        )
        high = lax.ppermute(lax.slice_in_dim(block, 0, width, axis=dim), axis, backward)
        block = jnp.concatenate([low, block, high], axis=dim)
    return block


def chain_kernel(data_ref, par_ref, out_ref, piv_ref, slv_ref):
    blocks, _, rows, width = data_ref.shape
    ns = par_ref[2:3, :]
    ls2 = par_ref[3:4, :]
    sp = par_ref[4:5, :]
    mps = par_ref[5:6, :]
    qs = par_ref[6:7, :]
    two_ls2 = 2.0 * ls2
    zeros = jnp.zeros_like(sp)
    carry = (zeros,) * 11
    for block in range(blocks):

        def forward(t, carry):
            inv, t0, t1, t2, t3, solved, c0, c1, c2, c3, logs = carry
            rough = data_ref[block, 0, pl.ds(t, 1), :]
            coup = data_ref[block, 1, pl.ds(t, 1), :]
            weight = data_ref[block, 2, pl.ds(t, 1), :]
            obs = data_ref[block, 3, pl.ds(t, 1), :]
            prior = sp * rough
            nugget = ns * weight
            diagonal = prior + nugget
            offdiag = mps * coup
            pivots = diagonal - offdiag * offdiag * inv
            ratios = offdiag * inv
            rr = ratios * ratios
            t0 = rr * t0 + 2.0 * prior - 4.0 * offdiag * ratios
            t1 = rr * t1 + prior - 2.0 * offdiag * ratios
            t2 = rr * t2 + qs * rough - two_ls2 * offdiag * ratios
            t3 = rr * t3 + nugget
            solved = obs - ratios * solved
            c0 = c0 + 0.5 * t0 / pivots
            c1 = c1 + 0.5 * t1 / pivots
            c2 = c2 + 0.5 * t2 / pivots
            c3 = c3 + 0.5 * t3 / pivots
            logs = logs + jnp.log(pivots)
            piv_ref[block, pl.ds(t, 1), :] = pivots
            slv_ref[block, pl.ds(t, 1), :] = solved
            return (1.0 / pivots, t0, t1, t2, t3, solved, c0, c1, c2, c3, logs)

        carry = lax.fori_loop(0, rows, forward, carry, unroll=8)
    c0, c1, c2, c3, logs = carry[6:]
    closing = (zeros,) * 5
    for block in reversed(range(blocks)):

        def backward(i, carry):
            t = rows - 1 - i
            following, q0, q1, q2, q3 = carry
            rough = data_ref[block, 0, pl.ds(t, 1), :]
            coup = data_ref[block, 1, pl.ds(t, 1), :]
            weight = data_ref[block, 2, pl.ds(t, 1), :]
            prior = sp * rough
            nugget = ns * weight
            offdiag = mps * coup
            values = (slv_ref[block, pl.ds(t, 1), :] - following) / piv_ref[block, pl.ds(t, 1), :]
            q0 = q0 + 2.0 * prior * values * values + 4.0 * values * following
            q1 = q1 + prior * values * values + 2.0 * values * following
            q2 = q2 + qs * rough * values * values + two_ls2 * values * following
            q3 = q3 + nugget * values * values
            out_ref[block, pl.ds(t, 1), :] = values
            return (offdiag * values, q0, q1, q2, q3)

        closing = lax.fori_loop(0, rows, backward, closing, unroll=8)
    q0, q1, q2, q3 = closing[1:]
    scale = 1.0 / (rows * blocks)
    stats = jnp.concatenate(
        [
            logs * scale,
            (c0 - 0.5 * q0) * scale,
            (c1 - 0.5 * q1) * scale,
            (c2 - 0.5 * q2) * scale,
            (c3 - 0.5 * q3) * scale,
            jnp.zeros((3, width), jnp.float32),
        ],
        axis=0,
    )
    for block in range(blocks):
        out_ref[block, rows : rows + 8, :] = stats


def run_chain(data, params):
    blocks, _, rows, width = data.shape
    vmem = pl.BlockSpec(memory_space=pltpu.VMEM)
    return pl.pallas_call(
        chain_kernel,
        out_shape=jax.ShapeDtypeStruct((blocks, rows + 8, width), jnp.float32),
        in_specs=[vmem, vmem],
        out_specs=vmem,
        scratch_shapes=[pltpu.VMEM((blocks, rows, width), jnp.float32)] * 2,
        interpret=INTERPRET,
    )(data, params)


def per_device(
    log_kappa,
    node_mass,
    rho_base,
    edge_weight,
    offsets,
    roughness,
    coupling,
    obs_weight,
    observed,
    hyper_params,
):
    row_count, full_width = roughness.shape
    time_count = lax.axis_size("tm")
    hyp_count = lax.axis_size("hyp")
    time_place = lax.axis_index("tm")
    hyp_place = lax.axis_index("hyp")
    quarter = full_width // hyp_count
    chunk = quarter // time_count
    first = hyp_place * quarter + time_place * chunk

    stacked = jnp.stack([roughness, coupling, obs_weight, observed])
    mine = lax.dynamic_slice_in_dim(stacked, hyp_place * quarter, quarter, axis=2)
    pieces = mine.reshape(4, row_count, time_count, chunk).transpose(2, 0, 1, 3)
    data = lax.all_to_all(pieces, "tm", 0, 0, tiled=True)

    kappa_sq = jnp.exp(2.0 * log_kappa)
    padded = with_halo(kappa_sq, (("space", 0),), BAND)
    window = lax.dynamic_slice_in_dim(padded, first, chunk + 2 * BAND)
    near_off = lax.dynamic_slice_in_dim(offsets, first, chunk, axis=1)
    weights = lax.dynamic_slice_in_dim(edge_weight, first, chunk, axis=1)
    mass = lax.dynamic_slice_in_dim(node_mass, first, chunk)
    base = lax.dynamic_slice_in_dim(rho_base, first, chunk)
    own_kappa = window[BAND : BAND + chunk]
    nearby = jnp.zeros(near_off.shape, jnp.float32)
    for shift in range(-BAND, BAND + 1):
        nearby = jnp.where(
            near_off == shift, window[None, BAND + shift : BAND + shift + chunk], nearby
        )
    spatial = jnp.exp(2.0 * hyper_params[0]) * (
        mass * own_kappa + jnp.sum(weights * nearby, axis=0)
    )
    scaled = jnp.exp(hyper_params[1]) * spatial
    persist = jnp.tanh(hyper_params[2] + base)
    nugget_scale = jnp.exp(hyper_params[3]) + jnp.zeros_like(persist)
    log_slope = (1.0 - persist * persist) / persist
    params = jnp.stack(
        [
            scaled,
            persist,
            nugget_scale,
            log_slope,
            scaled * (1.0 + persist * persist),
            -persist * scaled,
            2.0 * persist * (1.0 - persist * persist) * scaled,
            jnp.zeros_like(persist),
        ]
    )
    payload = run_chain(data, params)
    received = lax.all_to_all(payload, "tm", 0, 0, tiled=True)
    solution_out = received[:, :row_count].transpose(1, 0, 2).reshape(row_count, quarter)
    stats_quarter = received[:, row_count : row_count + 5].transpose(1, 0, 2).reshape(5, quarter)
    stats_full = lax.all_gather(stats_quarter, "hyp", axis=1, tiled=True)
    return (solution_out, stats_full[0], stats_full[1:5])


def solution(mesh):
    placed = (
        P("space"),
        P("space"),
        P("space"),
        P(None, "space"),
        P(None, "space"),
        P("tm", "space"),
        P("tm", "space"),
        P("tm", "space"),
        P("tm", "space"),
        P(),
    )
    return jax.shard_map(
        per_device,
        mesh=mesh,
        in_specs=placed,
        out_specs=(P("tm", ("space", "hyp")), P("space"), P(None, "space")),
        check_vma=False,
    )
```

```python
import jax
import jax.numpy as jnp
from jax import lax
from jax.experimental import pallas as pl
from jax.experimental.pallas import tpu as pltpu
from jax.sharding import PartitionSpec as P

BAND = 64
INTERPRET = False


def with_halo(block, sides, width):
    for axis, dim in sides:
        count = lax.axis_size(axis)
        forward = [(i, i + 1) for i in range(count - 1)]
        backward = [(target, source) for source, target in forward]
        low = lax.ppermute(
            lax.slice_in_dim(block, block.shape[dim] - width, None, axis=dim), axis, forward
        )
        high = lax.ppermute(lax.slice_in_dim(block, 0, width, axis=dim), axis, backward)
        block = jnp.concatenate([low, block, high], axis=dim)
    return block


def chain_kernel(place_ref, data_ref, par_ref, out_ref, piv_ref, slv_ref):
    blocks, _, rows, width = data_ref.shape
    place = place_ref[0]
    ns = par_ref[2:3, :]
    ls2 = par_ref[3:4, :]
    sp = par_ref[4:5, :]
    mps = par_ref[5:6, :]
    qs = par_ref[6:7, :]
    two_ls2 = 2.0 * ls2
    zeros = jnp.zeros_like(sp)
    carry = (zeros,) * 11
    for block in range(blocks):
        slot = lax.rem(place - block + blocks, blocks)

        def forward(t, carry):
            inv, t0, t1, t2, t3, solved, c0, c1, c2, c3, logs = carry
            rough = data_ref[slot, 0, pl.ds(t, 1), :]
            coup = data_ref[slot, 1, pl.ds(t, 1), :]
            weight = data_ref[slot, 2, pl.ds(t, 1), :]
            obs = data_ref[slot, 3, pl.ds(t, 1), :]
            prior = sp * rough
            nugget = ns * weight
            diagonal = prior + nugget
            offdiag = mps * coup
            pivots = diagonal - offdiag * offdiag * inv
            ratios = offdiag * inv
            rr = ratios * ratios
            t0 = rr * t0 + 2.0 * prior - 4.0 * offdiag * ratios
            t1 = rr * t1 + prior - 2.0 * offdiag * ratios
            t2 = rr * t2 + qs * rough - two_ls2 * offdiag * ratios
            t3 = rr * t3 + nugget
            solved = obs - ratios * solved
            c0 = c0 + 0.5 * t0 / pivots
            c1 = c1 + 0.5 * t1 / pivots
            c2 = c2 + 0.5 * t2 / pivots
            c3 = c3 + 0.5 * t3 / pivots
            logs = logs + jnp.log(pivots)
            piv_ref[block, pl.ds(t, 1), :] = pivots
            slv_ref[block, pl.ds(t, 1), :] = solved
            return (1.0 / pivots, t0, t1, t2, t3, solved, c0, c1, c2, c3, logs)

        carry = lax.fori_loop(0, rows, forward, carry, unroll=8)
    c0, c1, c2, c3, logs = carry[6:]
    closing = (zeros,) * 5
    for block in reversed(range(blocks)):
        slot = lax.rem(place - block + blocks, blocks)

        def backward(i, carry):
            t = rows - 1 - i
            following, q0, q1, q2, q3 = carry
            rough = data_ref[slot, 0, pl.ds(t, 1), :]
            coup = data_ref[slot, 1, pl.ds(t, 1), :]
            weight = data_ref[slot, 2, pl.ds(t, 1), :]
            prior = sp * rough
            nugget = ns * weight
            offdiag = mps * coup
            values = (slv_ref[block, pl.ds(t, 1), :] - following) / piv_ref[block, pl.ds(t, 1), :]
            q0 = q0 + 2.0 * prior * values * values + 4.0 * values * following
            q1 = q1 + prior * values * values + 2.0 * values * following
            q2 = q2 + qs * rough * values * values + two_ls2 * values * following
            q3 = q3 + nugget * values * values
            out_ref[block, pl.ds(t, 1), :] = values
            return (offdiag * values, q0, q1, q2, q3)

        closing = lax.fori_loop(0, rows, backward, closing, unroll=8)
    q0, q1, q2, q3 = closing[1:]
    scale = 1.0 / (rows * blocks)
    stats = jnp.concatenate(
        [
            logs * scale,
            (c0 - 0.5 * q0) * scale,
            (c1 - 0.5 * q1) * scale,
            (c2 - 0.5 * q2) * scale,
            (c3 - 0.5 * q3) * scale,
            jnp.zeros((3, width), jnp.float32),
        ],
        axis=0,
    )
    for block in range(blocks):
        out_ref[block, rows : rows + 8, :] = stats


def run_chain(place, data, params):
    blocks, _, rows, width = data.shape
    vmem = pl.BlockSpec(memory_space=pltpu.VMEM)
    smem = pl.BlockSpec(memory_space=pltpu.SMEM)
    return pl.pallas_call(
        chain_kernel,
        out_shape=jax.ShapeDtypeStruct((blocks, rows + 8, width), jnp.float32),
        in_specs=[smem, vmem, vmem],
        out_specs=vmem,
        scratch_shapes=[pltpu.VMEM((blocks, rows, width), jnp.float32)] * 2,
        interpret=INTERPRET,
    )(place, data, params)


def per_device(
    log_kappa,
    node_mass,
    rho_base,
    edge_weight,
    offsets,
    roughness,
    coupling,
    obs_weight,
    observed,
    hyper_params,
):
    row_count, full_width = roughness.shape
    time_count = lax.axis_size("tm")
    hyp_count = lax.axis_size("hyp")
    time_place = lax.axis_index("tm")
    hyp_place = lax.axis_index("hyp")
    quarter = full_width // hyp_count
    chunk = quarter // time_count
    first = hyp_place * quarter + time_place * chunk

    stacked = jnp.stack([roughness, coupling, obs_weight, observed])
    pieces = [
        lax.dynamic_slice_in_dim(
            stacked,
            hyp_place * quarter + lax.rem(time_place + shift, time_count) * chunk,
            chunk,
            axis=2,
        )
        for shift in range(time_count)
    ]
    arrived = [pieces[0]] + [
        lax.ppermute(
            pieces[shift],
            "tm",
            [(i, (i + shift) % time_count) for i in range(time_count)],
        )
        for shift in range(1, time_count)
    ]
    data = jnp.stack(arrived)
    place = time_place.astype(jnp.int32).reshape(1)

    kappa_sq = jnp.exp(2.0 * log_kappa)
    padded = with_halo(kappa_sq, (("space", 0),), BAND)
    window = lax.dynamic_slice_in_dim(padded, first, chunk + 2 * BAND)
    near_off = lax.dynamic_slice_in_dim(offsets, first, chunk, axis=1)
    weights = lax.dynamic_slice_in_dim(edge_weight, first, chunk, axis=1)
    mass = lax.dynamic_slice_in_dim(node_mass, first, chunk)
    base = lax.dynamic_slice_in_dim(rho_base, first, chunk)
    own_kappa = window[BAND : BAND + chunk]
    nearby = jnp.zeros(near_off.shape, jnp.float32)
    for shift in range(-BAND, BAND + 1):
        nearby = jnp.where(
            near_off == shift, window[None, BAND + shift : BAND + shift + chunk], nearby
        )
    spatial = jnp.exp(2.0 * hyper_params[0]) * (
        mass * own_kappa + jnp.sum(weights * nearby, axis=0)
    )
    scaled = jnp.exp(hyper_params[1]) * spatial
    persist = jnp.tanh(hyper_params[2] + base)
    nugget_scale = jnp.exp(hyper_params[3]) + jnp.zeros_like(persist)
    log_slope = (1.0 - persist * persist) / persist
    params = jnp.stack(
        [
            scaled,
            persist,
            nugget_scale,
            log_slope,
            scaled * (1.0 + persist * persist),
            -persist * scaled,
            2.0 * persist * (1.0 - persist * persist) * scaled,
            jnp.zeros_like(persist),
        ]
    )
    payload = run_chain(place, data, params)
    received = lax.all_to_all(payload, "tm", 0, 0, tiled=True)
    solution_out = received[:, :row_count].transpose(1, 0, 2).reshape(row_count, quarter)
    stats_quarter = received[:, row_count : row_count + 5].transpose(1, 0, 2).reshape(5, quarter)
    stats_full = lax.all_gather(stats_quarter, "hyp", axis=1, tiled=True)
    return (solution_out, stats_full[0], stats_full[1:5])


def solution(mesh):
    placed = (
        P("space"),
        P("space"),
        P("space"),
        P(None, "space"),
        P(None, "space"),
        P("tm", "space"),
        P("tm", "space"),
        P("tm", "space"),
        P("tm", "space"),
        P(),
    )
    return jax.shard_map(
        per_device,
        mesh=mesh,
        in_specs=placed,
        out_specs=(P("tm", ("space", "hyp")), P("space"), P(None, "space")),
        check_vma=False,
    )
```

```python
import jax
import jax.numpy as jnp
from jax import lax
from jax.experimental import pallas as pl
from jax.experimental.pallas import tpu as pltpu
from jax.sharding import PartitionSpec as P

BAND = 64
INTERPRET = False


def with_halo(block, axis, width):
    count = lax.axis_size(axis)
    if count == 2:
        place = lax.axis_index(axis)
        send = jnp.where(place == 0, block[-width:], block[:width])
        got = lax.ppermute(send, axis, [(0, 1), (1, 0)])
        low = jnp.where(place == 1, got, jnp.zeros_like(got))
        high = jnp.where(place == 0, got, jnp.zeros_like(got))
    else:
        forward = [(i, i + 1) for i in range(count - 1)]
        backward = [(target, source) for source, target in forward]
        low = lax.ppermute(block[-width:], axis, forward)
        high = lax.ppermute(block[:width], axis, backward)
    return jnp.concatenate([low, block, high])


def chain_kernel(place_ref, data_ref, par_ref, out_ref, piv_ref, slv_ref):
    blocks, _, rows, width = data_ref.shape
    place = place_ref[0]
    ns = par_ref[2:3, :]
    ls2 = par_ref[3:4, :]
    sp = par_ref[4:5, :]
    mps = par_ref[5:6, :]
    qs = par_ref[6:7, :]
    two_ls2 = 2.0 * ls2
    zeros = jnp.zeros_like(sp)
    carry = (zeros,) * 11
    for block in range(blocks):
        slot = lax.rem(place - block + blocks, blocks)

        def forward(t, carry):
            inv, t0, t1, t2, t3, solved, c0, c1, c2, c3, logs = carry
            rough = data_ref[slot, 0, pl.ds(t, 1), :]
            coup = data_ref[slot, 1, pl.ds(t, 1), :]
            weight = data_ref[slot, 2, pl.ds(t, 1), :]
            obs = data_ref[slot, 3, pl.ds(t, 1), :]
            prior = sp * rough
            nugget = ns * weight
            diagonal = prior + nugget
            offdiag = mps * coup
            pivots = diagonal - offdiag * offdiag * inv
            ratios = offdiag * inv
            rr = ratios * ratios
            t0 = rr * t0 + 2.0 * prior - 4.0 * offdiag * ratios
            t1 = rr * t1 + prior - 2.0 * offdiag * ratios
            t2 = rr * t2 + qs * rough - two_ls2 * offdiag * ratios
            t3 = rr * t3 + nugget
            solved = obs - ratios * solved
            c0 = c0 + 0.5 * t0 / pivots
            c1 = c1 + 0.5 * t1 / pivots
            c2 = c2 + 0.5 * t2 / pivots
            c3 = c3 + 0.5 * t3 / pivots
            logs = logs + jnp.log(pivots)
            piv_ref[block, pl.ds(t, 1), :] = pivots
            slv_ref[block, pl.ds(t, 1), :] = solved
            return (1.0 / pivots, t0, t1, t2, t3, solved, c0, c1, c2, c3, logs)

        carry = lax.fori_loop(0, rows, forward, carry, unroll=8)
    c0, c1, c2, c3, logs = carry[6:]
    closing = (zeros,) * 5
    for block in reversed(range(blocks)):
        slot = lax.rem(place - block + blocks, blocks)

        def backward(i, carry):
            t = rows - 1 - i
            following, q0, q1, q2, q3 = carry
            rough = data_ref[slot, 0, pl.ds(t, 1), :]
            coup = data_ref[slot, 1, pl.ds(t, 1), :]
            weight = data_ref[slot, 2, pl.ds(t, 1), :]
            prior = sp * rough
            nugget = ns * weight
            offdiag = mps * coup
            values = (slv_ref[block, pl.ds(t, 1), :] - following) / piv_ref[block, pl.ds(t, 1), :]
            q0 = q0 + 2.0 * prior * values * values + 4.0 * values * following
            q1 = q1 + prior * values * values + 2.0 * values * following
            q2 = q2 + qs * rough * values * values + two_ls2 * values * following
            q3 = q3 + nugget * values * values
            out_ref[block, pl.ds(t, 1), :] = values
            return (offdiag * values, q0, q1, q2, q3)

        closing = lax.fori_loop(0, rows, backward, closing, unroll=8)
    q0, q1, q2, q3 = closing[1:]
    scale = 1.0 / (rows * blocks)
    stats = jnp.concatenate(
        [
            logs * scale,
            (c0 - 0.5 * q0) * scale,
            (c1 - 0.5 * q1) * scale,
            (c2 - 0.5 * q2) * scale,
            (c3 - 0.5 * q3) * scale,
            jnp.zeros((3, width), jnp.float32),
        ],
        axis=0,
    )
    for block in range(blocks):
        out_ref[block, rows : rows + 8, :] = stats


def run_chain(place, data, params):
    blocks, _, rows, width = data.shape
    vmem = pl.BlockSpec(memory_space=pltpu.VMEM)
    smem = pl.BlockSpec(memory_space=pltpu.SMEM)
    return pl.pallas_call(
        chain_kernel,
        out_shape=jax.ShapeDtypeStruct((blocks, rows + 8, width), jnp.float32),
        in_specs=[smem, vmem, vmem],
        out_specs=vmem,
        scratch_shapes=[pltpu.VMEM((blocks, rows, width), jnp.float32)] * 2,
        interpret=INTERPRET,
    )(place, data, params)


def per_device_body(
    log_kappa,
    node_mass,
    rho_base,
    edge_weight,
    offsets,
    roughness,
    coupling,
    obs_weight,
    observed,
    hyper_params,
):
    row_count, full_width = roughness.shape
    time_count = lax.axis_size("tm")
    hyp_count = lax.axis_size("hyp")
    time_place = lax.axis_index("tm")
    hyp_place = lax.axis_index("hyp")
    quarter = full_width // hyp_count
    chunk = quarter // time_count
    first = hyp_place * quarter + time_place * chunk

    kappa_sq = jnp.exp(2.0 * log_kappa)
    padded = with_halo(kappa_sq, "space", BAND)

    stacked = jnp.stack([roughness, coupling, obs_weight, observed])
    pieces = [
        lax.dynamic_slice_in_dim(
            stacked,
            hyp_place * quarter + lax.rem(time_place + shift, time_count) * chunk,
            chunk,
            axis=2,
        )
        for shift in range(time_count)
    ]
    arrived = [pieces[0]] + [
        lax.ppermute(
            pieces[shift],
            "tm",
            [(i, (i + shift) % time_count) for i in range(time_count)],
        )
        for shift in range(1, time_count)
    ]
    data = jnp.stack(arrived)
    place = time_place.astype(jnp.int32).reshape(1)

    window = lax.dynamic_slice_in_dim(padded, first, chunk + 2 * BAND)
    near_off = lax.dynamic_slice_in_dim(offsets, first, chunk, axis=1)
    weights = lax.dynamic_slice_in_dim(edge_weight, first, chunk, axis=1)
    mass = lax.dynamic_slice_in_dim(node_mass, first, chunk)
    base = lax.dynamic_slice_in_dim(rho_base, first, chunk)
    own_kappa = window[BAND : BAND + chunk]
    nearby = jnp.zeros(near_off.shape, jnp.float32)
    for shift in range(-BAND, BAND + 1):
        nearby = jnp.where(
            near_off == shift, window[None, BAND + shift : BAND + shift + chunk], nearby
        )
    spatial = jnp.exp(2.0 * hyper_params[0]) * (
        mass * own_kappa + jnp.sum(weights * nearby, axis=0)
    )
    scaled = jnp.exp(hyper_params[1]) * spatial
    persist = jnp.tanh(hyper_params[2] + base)
    nugget_scale = jnp.exp(hyper_params[3]) + jnp.zeros_like(persist)
    log_slope = (1.0 - persist * persist) / persist
    params = jnp.stack(
        [
            scaled,
            persist,
            nugget_scale,
            log_slope,
            scaled * (1.0 + persist * persist),
            -persist * scaled,
            2.0 * persist * (1.0 - persist * persist) * scaled,
            jnp.zeros_like(persist),
        ]
    )
    payload = run_chain(place, data, params)
    received = lax.all_to_all(payload, "tm", 0, 0, tiled=True)
    solution_out = received[:, :row_count].transpose(1, 0, 2).reshape(row_count, quarter)
    stats_quarter = received[:, row_count : row_count + 5].transpose(1, 0, 2).reshape(5, quarter)
    stats_full = lax.all_gather(stats_quarter, "hyp", axis=1, tiled=True)
    return (solution_out, stats_full[0], stats_full[1:5])


def solution(mesh):
    placed = (
        P("space"),
        P("space"),
        P("space"),
        P(None, "space"),
        P(None, "space"),
        P("tm", "space"),
        P("tm", "space"),
        P("tm", "space"),
        P("tm", "space"),
        P(),
    )
    return jax.shard_map(
        per_device_body,
        mesh=mesh,
        in_specs=placed,
        out_specs=(P("tm", ("space", "hyp")), P("space"), P(None, "space")),
        check_vma=False,
    )
```

```python
import jax
import jax.numpy as jnp
from jax import lax
from jax.experimental import pallas as pl
from jax.experimental.pallas import tpu as pltpu
from jax.sharding import PartitionSpec as P

BAND = 64
INTERPRET = False


def with_halo(block, axis, width):
    count = lax.axis_size(axis)
    if count == 2:
        place = lax.axis_index(axis)
        send = jnp.where(place == 0, block[-width:], block[:width])
        got = lax.ppermute(send, axis, [(0, 1), (1, 0)])
        low = jnp.where(place == 1, got, jnp.zeros_like(got))
        high = jnp.where(place == 0, got, jnp.zeros_like(got))
    else:
        forward = [(i, i + 1) for i in range(count - 1)]
        backward = [(target, source) for source, target in forward]
        low = lax.ppermute(block[-width:], axis, forward)
        high = lax.ppermute(block[:width], axis, backward)
    return jnp.concatenate([low, block, high])


def chain_kernel(
    place_ref, hyper_ref, window_ref, offsets_ref, weights_ref, node_ref, data_ref,
    out_ref, piv_ref, slv_ref,
):
    blocks, _, rows, width = data_ref.shape
    place = place_ref[0]
    window = window_ref[...]
    span = window.shape[1]
    near_off = offsets_ref[...]
    nearby = jnp.zeros(near_off.shape, jnp.float32)
    own_kappa = None
    for shift in range(-BAND, BAND + 1):
        moved = pltpu.roll(window, (span - BAND - shift) % span, 1)[:, :width]
        if shift == 0:
            own_kappa = moved
        nearby = jnp.where(near_off == shift, moved, nearby)
    weights = weights_ref[...]
    edge_sum = (
        weights[0:1] * nearby[0:1]
        + weights[1:2] * nearby[1:2]
        + weights[2:3] * nearby[2:3]
        + weights[3:4] * nearby[3:4]
    )
    spatial = hyper_ref[0] * (node_ref[0:1, :] * own_kappa + edge_sum)
    scaled = hyper_ref[1] * spatial
    persist = jnp.tanh(hyper_ref[2] + node_ref[1:2, :])
    ns = jnp.zeros_like(persist) + hyper_ref[3]
    ls2 = (1.0 - persist * persist) / persist
    sp = scaled * (1.0 + persist * persist)
    mps = -persist * scaled
    qs = 2.0 * persist * (1.0 - persist * persist) * scaled
    two_ls2 = 2.0 * ls2
    zeros = jnp.zeros_like(sp)
    carry = (zeros,) * 11
    for block in range(blocks):
        slot = lax.rem(place - block + blocks, blocks)

        def forward(t, carry):
            inv, t0, t1, t2, t3, solved, c0, c1, c2, c3, logs = carry
            rough = data_ref[slot, 0, pl.ds(t, 1), :]
            coup = data_ref[slot, 1, pl.ds(t, 1), :]
            weight = data_ref[slot, 2, pl.ds(t, 1), :]
            obs = data_ref[slot, 3, pl.ds(t, 1), :]
            prior = sp * rough
            nugget = ns * weight
            diagonal = prior + nugget
            offdiag = mps * coup
            pivots = diagonal - offdiag * offdiag * inv
            ratios = offdiag * inv
            rr = ratios * ratios
            t0 = rr * t0 + 2.0 * prior - 4.0 * offdiag * ratios
            t1 = rr * t1 + prior - 2.0 * offdiag * ratios
            t2 = rr * t2 + qs * rough - two_ls2 * offdiag * ratios
            t3 = rr * t3 + nugget
            solved = obs - ratios * solved
            c0 = c0 + 0.5 * t0 / pivots
            c1 = c1 + 0.5 * t1 / pivots
            c2 = c2 + 0.5 * t2 / pivots
            c3 = c3 + 0.5 * t3 / pivots
            logs = logs + jnp.log(pivots)
            piv_ref[block, pl.ds(t, 1), :] = pivots
            slv_ref[block, pl.ds(t, 1), :] = solved
            return (1.0 / pivots, t0, t1, t2, t3, solved, c0, c1, c2, c3, logs)

        carry = lax.fori_loop(0, rows, forward, carry, unroll=8)
    c0, c1, c2, c3, logs = carry[6:]
    closing = (zeros,) * 5
    for block in reversed(range(blocks)):
        slot = lax.rem(place - block + blocks, blocks)

        def backward(i, carry):
            t = rows - 1 - i
            following, q0, q1, q2, q3 = carry
            rough = data_ref[slot, 0, pl.ds(t, 1), :]
            coup = data_ref[slot, 1, pl.ds(t, 1), :]
            weight = data_ref[slot, 2, pl.ds(t, 1), :]
            prior = sp * rough
            nugget = ns * weight
            offdiag = mps * coup
            values = (slv_ref[block, pl.ds(t, 1), :] - following) / piv_ref[block, pl.ds(t, 1), :]
            q0 = q0 + 2.0 * prior * values * values + 4.0 * values * following
            q1 = q1 + prior * values * values + 2.0 * values * following
            q2 = q2 + qs * rough * values * values + two_ls2 * values * following
            q3 = q3 + nugget * values * values
            out_ref[block, pl.ds(t, 1), :] = values
            return (offdiag * values, q0, q1, q2, q3)

        closing = lax.fori_loop(0, rows, backward, closing, unroll=8)
    q0, q1, q2, q3 = closing[1:]
    scale = 1.0 / (rows * blocks)
    stats = jnp.concatenate(
        [
            logs * scale,
            (c0 - 0.5 * q0) * scale,
            (c1 - 0.5 * q1) * scale,
            (c2 - 0.5 * q2) * scale,
            (c3 - 0.5 * q3) * scale,
            jnp.zeros((3, width), jnp.float32),
        ],
        axis=0,
    )
    for block in range(blocks):
        out_ref[block, rows : rows + 8, :] = stats


def run_chain(place, hyper, window, near_off, weights, node, data):
    blocks, _, rows, width = data.shape
    vmem = pl.BlockSpec(memory_space=pltpu.VMEM)
    smem = pl.BlockSpec(memory_space=pltpu.SMEM)
    return pl.pallas_call(
        chain_kernel,
        out_shape=jax.ShapeDtypeStruct((blocks, rows + 8, width), jnp.float32),
        in_specs=[smem, smem, vmem, vmem, vmem, vmem, vmem],
        out_specs=vmem,
        scratch_shapes=[pltpu.VMEM((blocks, rows, width), jnp.float32)] * 2,
        interpret=INTERPRET,
    )(place, hyper, window, near_off, weights, node, data)


def per_device_body(
    log_kappa,
    node_mass,
    rho_base,
    edge_weight,
    offsets,
    roughness,
    coupling,
    obs_weight,
    observed,
    hyper_params,
):
    row_count, full_width = roughness.shape
    time_count = lax.axis_size("tm")
    hyp_count = lax.axis_size("hyp")
    time_place = lax.axis_index("tm")
    hyp_place = lax.axis_index("hyp")
    quarter = full_width // hyp_count
    chunk = quarter // time_count
    first = hyp_place * quarter + time_place * chunk

    kappa_sq = jnp.exp(2.0 * log_kappa)
    padded = with_halo(kappa_sq, "space", BAND)

    stacked = jnp.stack([roughness, coupling, obs_weight, observed])
    pieces = [
        lax.dynamic_slice_in_dim(
            stacked,
            hyp_place * quarter + lax.rem(time_place + shift, time_count) * chunk,
            chunk,
            axis=2,
        )
        for shift in range(time_count)
    ]
    arrived = [pieces[0]] + [
        lax.ppermute(
            pieces[shift],
            "tm",
            [(i, (i + shift) % time_count) for i in range(time_count)],
        )
        for shift in range(1, time_count)
    ]
    data = jnp.stack(arrived)
    place = time_place.astype(jnp.int32).reshape(1)

    window = lax.dynamic_slice_in_dim(padded, first, chunk + 2 * BAND)[None]
    near_off = lax.dynamic_slice_in_dim(offsets, first, chunk, axis=1)
    weights = lax.dynamic_slice_in_dim(edge_weight, first, chunk, axis=1)
    node = lax.dynamic_slice_in_dim(jnp.stack([node_mass, rho_base]), first, chunk, axis=1)
    hyper = jnp.stack(
        [
            jnp.exp(2.0 * hyper_params[0]),
            jnp.exp(hyper_params[1]),
            hyper_params[2],
            jnp.exp(hyper_params[3]),
        ]
    )
    payload = run_chain(place, hyper, window, near_off, weights, node, data)
    received = lax.all_to_all(payload, "tm", 0, 0, tiled=True)
    solution_out = received[:, :row_count].transpose(1, 0, 2).reshape(row_count, quarter)
    stats_quarter = received[:, row_count : row_count + 5].transpose(1, 0, 2).reshape(5, quarter)
    stats_full = lax.all_gather(stats_quarter, "hyp", axis=1, tiled=True)
    return (solution_out, stats_full[0], stats_full[1:5])


def solution(mesh):
    placed = (
        P("space"),
        P("space"),
        P("space"),
        P(None, "space"),
        P(None, "space"),
        P("tm", "space"),
        P("tm", "space"),
        P("tm", "space"),
        P("tm", "space"),
        P(),
    )
    return jax.shard_map(
        per_device_body,
        mesh=mesh,
        in_specs=placed,
        out_specs=(P("tm", ("space", "hyp")), P("space"), P(None, "space")),
        check_vma=False,
    )
```

```python
import functools

import jax
import jax.numpy as jnp
from jax import lax
from jax.experimental import pallas as pl
from jax.experimental.pallas import tpu as pltpu
from jax.sharding import PartitionSpec as P

BAND = 64
INTERPRET = False


def with_halo(block, axis, width):
    count = lax.axis_size(axis)
    if count == 2:
        place = lax.axis_index(axis)
        send = jnp.where(place == 0, block[-width:], block[:width])
        got = lax.ppermute(send, axis, [(0, 1), (1, 0)])
        low = jnp.where(place == 1, got, jnp.zeros_like(got))
        high = jnp.where(place == 0, got, jnp.zeros_like(got))
    else:
        forward = [(i, i + 1) for i in range(count - 1)]
        backward = [(target, source) for source, target in forward]
        low = lax.ppermute(block[-width:], axis, forward)
        high = lax.ppermute(block[:width], axis, backward)
    return jnp.concatenate([low, block, high])


def chain_kernel(*refs, aligned):
    place_ref, hyper_ref, window_ref, nodes_hbm, offsets_hbm = refs[:5]
    blocks = len(refs) - 12
    pieces = refs[5 : 5 + blocks]
    out_ref, piv_ref, slv_ref, data_ref, nodes_ref, offsets_ref, sems = refs[5 + blocks :]
    _, _, rows, width = data_ref.shape
    first = pl.multiple_of(place_ref[1], 128) if aligned else 0
    node_copy = pltpu.make_async_copy(nodes_hbm.at[:, pl.ds(first, width)], nodes_ref, sems.at[0])
    offsets_copy = pltpu.make_async_copy(
        offsets_hbm.at[:, pl.ds(first, width)], offsets_ref, sems.at[1]
    )
    node_copy.start()
    offsets_copy.start()
    for shift in range(blocks):
        data_ref[shift] = pieces[shift][...]
    node_copy.wait()
    offsets_copy.wait()

    place = place_ref[0]
    window = window_ref[...]
    span = window.shape[1]
    near_off = offsets_ref[...]
    ones = jnp.ones((1, width), jnp.float32)
    nearby = jnp.zeros(near_off.shape, jnp.float32)
    own_kappa = None
    for shift in range(-BAND, BAND + 1):
        moved = pltpu.roll(window, (span - BAND - shift) % span, 1)[:, :width]
        if shift == 0:
            own_kappa = moved
        nearby = jnp.where(near_off == shift, moved, nearby)
    weights = nodes_ref[2:6, :]
    edge_sum = (
        weights[0:1] * nearby[0:1]
        + weights[1:2] * nearby[1:2]
        + weights[2:3] * nearby[2:3]
        + weights[3:4] * nearby[3:4]
    )
    spatial = jnp.exp(2.0 * hyper_ref[0] * ones) * (nodes_ref[0:1, :] * own_kappa + edge_sum)
    scaled = jnp.exp(hyper_ref[1] * ones) * spatial
    persist = jnp.tanh(hyper_ref[2] + nodes_ref[1:2, :])
    ns = jnp.exp(hyper_ref[3] * ones)
    ls2 = (1.0 - persist * persist) / persist
    sp = scaled * (1.0 + persist * persist)
    mps = -persist * scaled
    qs = 2.0 * persist * (1.0 - persist * persist) * scaled
    two_ls2 = 2.0 * ls2
    zeros = jnp.zeros_like(sp)
    carry = (zeros,) * 11
    for block in range(blocks):
        slot = lax.rem(place - block + blocks, blocks)

        def forward(t, carry):
            inv, t0, t1, t2, t3, solved, c0, c1, c2, c3, logs = carry
            rough = data_ref[slot, 0, pl.ds(t, 1), :]
            coup = data_ref[slot, 1, pl.ds(t, 1), :]
            weight = data_ref[slot, 2, pl.ds(t, 1), :]
            obs = data_ref[slot, 3, pl.ds(t, 1), :]
            prior = sp * rough
            nugget = ns * weight
            diagonal = prior + nugget
            offdiag = mps * coup
            pivots = diagonal - offdiag * offdiag * inv
            ratios = offdiag * inv
            rr = ratios * ratios
            t0 = rr * t0 + 2.0 * prior - 4.0 * offdiag * ratios
            t1 = rr * t1 + prior - 2.0 * offdiag * ratios
            t2 = rr * t2 + qs * rough - two_ls2 * offdiag * ratios
            t3 = rr * t3 + nugget
            solved = obs - ratios * solved
            c0 = c0 + 0.5 * t0 / pivots
            c1 = c1 + 0.5 * t1 / pivots
            c2 = c2 + 0.5 * t2 / pivots
            c3 = c3 + 0.5 * t3 / pivots
            logs = logs + jnp.log(pivots)
            piv_ref[block, pl.ds(t, 1), :] = pivots
            slv_ref[block, pl.ds(t, 1), :] = solved
            return (1.0 / pivots, t0, t1, t2, t3, solved, c0, c1, c2, c3, logs)

        carry = lax.fori_loop(0, rows, forward, carry, unroll=8)
    c0, c1, c2, c3, logs = carry[6:]
    closing = (zeros,) * 5
    for block in reversed(range(blocks)):
        slot = lax.rem(place - block + blocks, blocks)

        def backward(i, carry):
            t = rows - 1 - i
            following, q0, q1, q2, q3 = carry
            rough = data_ref[slot, 0, pl.ds(t, 1), :]
            coup = data_ref[slot, 1, pl.ds(t, 1), :]
            weight = data_ref[slot, 2, pl.ds(t, 1), :]
            prior = sp * rough
            nugget = ns * weight
            offdiag = mps * coup
            values = (slv_ref[block, pl.ds(t, 1), :] - following) / piv_ref[block, pl.ds(t, 1), :]
            q0 = q0 + 2.0 * prior * values * values + 4.0 * values * following
            q1 = q1 + prior * values * values + 2.0 * values * following
            q2 = q2 + qs * rough * values * values + two_ls2 * values * following
            q3 = q3 + nugget * values * values
            out_ref[block, pl.ds(t, 1), :] = values
            return (offdiag * values, q0, q1, q2, q3)

        closing = lax.fori_loop(0, rows, backward, closing, unroll=8)
    q0, q1, q2, q3 = closing[1:]
    scale = 1.0 / (rows * blocks)
    stats = jnp.concatenate(
        [
            logs * scale,
            (c0 - 0.5 * q0) * scale,
            (c1 - 0.5 * q1) * scale,
            (c2 - 0.5 * q2) * scale,
            (c3 - 0.5 * q3) * scale,
            jnp.zeros((3, width), jnp.float32),
        ],
        axis=0,
    )
    for block in range(blocks):
        out_ref[block, rows : rows + 8, :] = stats


def run_chain(place, hyper, window, nodes, offsets, pieces):
    blocks = len(pieces)
    _, rows, width = pieces[0].shape
    vmem = pl.BlockSpec(memory_space=pltpu.VMEM)
    smem = pl.BlockSpec(memory_space=pltpu.SMEM)
    hbm = pl.BlockSpec(memory_space=pl.ANY)
    return pl.pallas_call(
        functools.partial(chain_kernel, aligned=nodes.shape[1] != width),
        out_shape=jax.ShapeDtypeStruct((blocks, rows + 8, width), jnp.float32),
        in_specs=[smem, smem, vmem, hbm, hbm] + [vmem] * blocks,
        out_specs=vmem,
        scratch_shapes=[
            pltpu.VMEM((blocks, rows, width), jnp.float32),
            pltpu.VMEM((blocks, rows, width), jnp.float32),
            pltpu.VMEM((blocks, 4, rows, width), jnp.float32),
            pltpu.VMEM((6, width), jnp.float32),
            pltpu.VMEM((4, width), jnp.int32),
            pltpu.SemaphoreType.DMA((2,)),
        ],
        interpret=INTERPRET,
    )(place, hyper, window, nodes, offsets, *pieces)


def per_device_body(
    log_kappa,
    node_mass,
    rho_base,
    edge_weight,
    offsets,
    roughness,
    coupling,
    obs_weight,
    observed,
    hyper_params,
):
    row_count, full_width = roughness.shape
    time_count = lax.axis_size("tm")
    hyp_count = lax.axis_size("hyp")
    time_place = lax.axis_index("tm")
    hyp_place = lax.axis_index("hyp")
    quarter = full_width // hyp_count
    chunk = quarter // time_count
    first = hyp_place * quarter + time_place * chunk

    kappa_sq = jnp.exp(2.0 * log_kappa)
    padded = with_halo(kappa_sq, "space", BAND)

    stacked = jnp.stack([roughness, coupling, obs_weight, observed])
    pieces = [
        lax.dynamic_slice_in_dim(
            stacked,
            hyp_place * quarter + lax.rem(time_place + shift, time_count) * chunk,
            chunk,
            axis=2,
        )
        for shift in range(time_count)
    ]
    arrived = [pieces[0]] + [
        lax.ppermute(
            pieces[shift],
            "tm",
            [(i, (i + shift) % time_count) for i in range(time_count)],
        )
        for shift in range(1, time_count)
    ]
    place = jnp.stack([time_place, first]).astype(jnp.int32)
    window = lax.dynamic_slice_in_dim(padded, first, chunk + 2 * BAND)[None]
    nodes = jnp.concatenate([node_mass[None], rho_base[None], edge_weight], axis=0)
    near_off = offsets
    if chunk % 128:
        nodes = lax.dynamic_slice_in_dim(nodes, first, chunk, axis=1)
        near_off = lax.dynamic_slice_in_dim(offsets, first, chunk, axis=1)
    payload = run_chain(place, hyper_params, window, nodes, near_off, arrived)
    received = lax.all_to_all(payload, "tm", 0, 0, tiled=True)
    solution_out = received[:, :row_count].transpose(1, 0, 2).reshape(row_count, quarter)
    stats_quarter = received[:, row_count : row_count + 5].transpose(1, 0, 2).reshape(5, quarter)
    stats_full = lax.all_gather(stats_quarter, "hyp", axis=1, tiled=True)
    return (solution_out, stats_full[0], stats_full[1:5])


def solution(mesh):
    placed = (
        P("space"),
        P("space"),
        P("space"),
        P(None, "space"),
        P(None, "space"),
        P("tm", "space"),
        P("tm", "space"),
        P("tm", "space"),
        P("tm", "space"),
        P(),
    )
    return jax.shard_map(
        per_device_body,
        mesh=mesh,
        in_specs=placed,
        out_specs=(P("tm", ("space", "hyp")), P("space"), P(None, "space")),
        check_vma=False,
    )
```

```python
import functools

import jax
import jax.numpy as jnp
from jax import lax
from jax.experimental import pallas as pl
from jax.experimental.pallas import tpu as pltpu
from jax.sharding import PartitionSpec as P

BAND = 64
INTERPRET = False


def with_halo(block, axis, width):
    count = lax.axis_size(axis)
    if count == 2:
        place = lax.axis_index(axis)
        send = jnp.where(place == 0, block[-width:], block[:width])
        got = lax.ppermute(send, axis, [(0, 1), (1, 0)])
        low = jnp.where(place == 1, got, jnp.zeros_like(got))
        high = jnp.where(place == 0, got, jnp.zeros_like(got))
    else:
        forward = [(i, i + 1) for i in range(count - 1)]
        backward = [(target, source) for source, target in forward]
        low = lax.ppermute(block[-width:], axis, forward)
        high = lax.ppermute(block[:width], axis, backward)
    return jnp.concatenate([low, block, high])


def chain_kernel(*refs, aligned):
    place_ref, hyper_ref, window_ref, nodes_hbm, offsets_hbm = refs[:5]
    blocks = len(refs) - 13
    pieces = refs[5 : 5 + blocks]
    out_ref, piv_ref, slv_ref, data_ref, nodes_ref, offsets_ref, sems, piece_sems = refs[5 + blocks :]
    _, _, rows, width = data_ref.shape
    first = pl.multiple_of(place_ref[1], 128) if aligned else 0
    node_copy = pltpu.make_async_copy(nodes_hbm.at[:, pl.ds(first, width)], nodes_ref, sems.at[0])
    offsets_copy = pltpu.make_async_copy(
        offsets_hbm.at[:, pl.ds(first, width)], offsets_ref, sems.at[1]
    )
    piece_copies = [
        pltpu.make_async_copy(pieces[shift], data_ref.at[shift], piece_sems.at[shift])
        for shift in range(blocks)
    ]
    node_copy.start()
    offsets_copy.start()
    for copy in piece_copies:
        copy.start()
    node_copy.wait()
    offsets_copy.wait()

    place = place_ref[0]
    window = window_ref[...]
    span = window.shape[1]
    near_off = offsets_ref[...]
    ones = jnp.ones((1, width), jnp.float32)
    nearby = jnp.zeros(near_off.shape, jnp.float32)
    own_kappa = None
    for shift in range(-BAND, BAND + 1):
        moved = pltpu.roll(window, (span - BAND - shift) % span, 1)[:, :width]
        if shift == 0:
            own_kappa = moved
        nearby = jnp.where(near_off == shift, moved, nearby)
    weights = nodes_ref[2:6, :]
    edge_sum = (
        weights[0:1] * nearby[0:1]
        + weights[1:2] * nearby[1:2]
        + weights[2:3] * nearby[2:3]
        + weights[3:4] * nearby[3:4]
    )
    spatial = jnp.exp(2.0 * hyper_ref[0] * ones) * (nodes_ref[0:1, :] * own_kappa + edge_sum)
    scaled = jnp.exp(hyper_ref[1] * ones) * spatial
    persist = jnp.tanh(hyper_ref[2] + nodes_ref[1:2, :])
    ns = jnp.exp(hyper_ref[3] * ones)
    ls2 = (1.0 - persist * persist) / persist
    sp = scaled * (1.0 + persist * persist)
    mps = -persist * scaled
    qs = 2.0 * persist * (1.0 - persist * persist) * scaled
    two_ls2 = 2.0 * ls2
    zeros = jnp.zeros_like(sp)
    carry = (zeros,) * 11
    for copy in piece_copies:
        copy.wait()
    for block in range(blocks):
        slot = lax.rem(place - block + blocks, blocks)

        def forward(t, carry):
            inv, t0, t1, t2, t3, solved, c0, c1, c2, c3, logs = carry
            rough = data_ref[slot, 0, pl.ds(t, 1), :]
            coup = data_ref[slot, 1, pl.ds(t, 1), :]
            weight = data_ref[slot, 2, pl.ds(t, 1), :]
            obs = data_ref[slot, 3, pl.ds(t, 1), :]
            prior = sp * rough
            nugget = ns * weight
            diagonal = prior + nugget
            offdiag = mps * coup
            pivots = diagonal - offdiag * offdiag * inv
            ratios = offdiag * inv
            rr = ratios * ratios
            t0 = rr * t0 + 2.0 * prior - 4.0 * offdiag * ratios
            t1 = rr * t1 + prior - 2.0 * offdiag * ratios
            t2 = rr * t2 + qs * rough - two_ls2 * offdiag * ratios
            t3 = rr * t3 + nugget
            solved = obs - ratios * solved
            inv = 1.0 / pivots
            c0 = c0 + 0.5 * t0 * inv
            c1 = c1 + 0.5 * t1 * inv
            c2 = c2 + 0.5 * t2 * inv
            c3 = c3 + 0.5 * t3 * inv
            logs = logs + jnp.log(pivots)
            piv_ref[block, pl.ds(t, 1), :] = inv
            slv_ref[block, pl.ds(t, 1), :] = solved
            return (inv, t0, t1, t2, t3, solved, c0, c1, c2, c3, logs)

        carry = lax.fori_loop(0, rows, forward, carry, unroll=8)
    c0, c1, c2, c3, logs = carry[6:]
    closing = (zeros,) * 5
    for block in reversed(range(blocks)):
        slot = lax.rem(place - block + blocks, blocks)

        def backward(i, carry):
            t = rows - 1 - i
            following, q0, q1, q2, q3 = carry
            rough = data_ref[slot, 0, pl.ds(t, 1), :]
            coup = data_ref[slot, 1, pl.ds(t, 1), :]
            weight = data_ref[slot, 2, pl.ds(t, 1), :]
            prior = sp * rough
            nugget = ns * weight
            offdiag = mps * coup
            values = (slv_ref[block, pl.ds(t, 1), :] - following) * piv_ref[block, pl.ds(t, 1), :]
            q0 = q0 + 2.0 * prior * values * values + 4.0 * values * following
            q1 = q1 + prior * values * values + 2.0 * values * following
            q2 = q2 + qs * rough * values * values + two_ls2 * values * following
            q3 = q3 + nugget * values * values
            out_ref[block, pl.ds(t, 1), :] = values
            return (offdiag * values, q0, q1, q2, q3)

        closing = lax.fori_loop(0, rows, backward, closing, unroll=8)
    q0, q1, q2, q3 = closing[1:]
    scale = 1.0 / (rows * blocks)
    stats = jnp.concatenate(
        [
            logs * scale,
            (c0 - 0.5 * q0) * scale,
            (c1 - 0.5 * q1) * scale,
            (c2 - 0.5 * q2) * scale,
            (c3 - 0.5 * q3) * scale,
            jnp.zeros((3, width), jnp.float32),
        ],
        axis=0,
    )
    for block in range(blocks):
        out_ref[block, rows : rows + 8, :] = stats


def run_chain(place, hyper, window, nodes, offsets, pieces):
    blocks = len(pieces)
    _, rows, width = pieces[0].shape
    vmem = pl.BlockSpec(memory_space=pltpu.VMEM)
    smem = pl.BlockSpec(memory_space=pltpu.SMEM)
    hbm = pl.BlockSpec(memory_space=pl.ANY)
    return pl.pallas_call(
        functools.partial(chain_kernel, aligned=nodes.shape[1] != width),
        out_shape=jax.ShapeDtypeStruct((blocks, rows + 8, width), jnp.float32),
        in_specs=[smem, smem, vmem, hbm, hbm] + [hbm] * blocks,
        out_specs=vmem,
        scratch_shapes=[
            pltpu.VMEM((blocks, rows, width), jnp.float32),
            pltpu.VMEM((blocks, rows, width), jnp.float32),
            pltpu.VMEM((blocks, 4, rows, width), jnp.float32),
            pltpu.VMEM((6, width), jnp.float32),
            pltpu.VMEM((4, width), jnp.int32),
            pltpu.SemaphoreType.DMA((2,)),
            pltpu.SemaphoreType.DMA((blocks,)),
        ],
        interpret=INTERPRET,
    )(place, hyper, window, nodes, offsets, *pieces)


def per_device_body(
    log_kappa,
    node_mass,
    rho_base,
    edge_weight,
    offsets,
    roughness,
    coupling,
    obs_weight,
    observed,
    hyper_params,
):
    row_count, full_width = roughness.shape
    time_count = lax.axis_size("tm")
    hyp_count = lax.axis_size("hyp")
    time_place = lax.axis_index("tm")
    hyp_place = lax.axis_index("hyp")
    quarter = full_width // hyp_count
    chunk = quarter // time_count
    first = hyp_place * quarter + time_place * chunk

    kappa_sq = jnp.exp(2.0 * log_kappa)
    padded = with_halo(kappa_sq, "space", BAND)

    stacked = jnp.stack([roughness, coupling, obs_weight, observed])
    pieces = [
        lax.dynamic_slice_in_dim(
            stacked,
            hyp_place * quarter + lax.rem(time_place + shift, time_count) * chunk,
            chunk,
            axis=2,
        )
        for shift in range(time_count)
    ]
    arrived = [pieces[0]] + [
        lax.ppermute(
            pieces[shift],
            "tm",
            [(i, (i + shift) % time_count) for i in range(time_count)],
        )
        for shift in range(1, time_count)
    ]
    place = jnp.stack([time_place, first]).astype(jnp.int32)
    window = lax.dynamic_slice_in_dim(padded, first, chunk + 2 * BAND)[None]
    nodes = jnp.concatenate([node_mass[None], rho_base[None], edge_weight], axis=0)
    near_off = offsets
    if chunk % 128:
        nodes = lax.dynamic_slice_in_dim(nodes, first, chunk, axis=1)
        near_off = lax.dynamic_slice_in_dim(offsets, first, chunk, axis=1)
    payload = run_chain(place, hyper_params, window, nodes, near_off, arrived)
    received = lax.all_to_all(payload, "tm", 0, 0, tiled=True)
    solution_out = received[:, :row_count].transpose(1, 0, 2).reshape(row_count, quarter)
    stats_quarter = received[:, row_count : row_count + 5].transpose(1, 0, 2).reshape(5, quarter)
    stats_full = lax.all_gather(stats_quarter, "hyp", axis=1, tiled=True)
    return (solution_out, stats_full[0], stats_full[1:5])


def solution(mesh):
    placed = (
        P("space"),
        P("space"),
        P("space"),
        P(None, "space"),
        P(None, "space"),
        P("tm", "space"),
        P("tm", "space"),
        P("tm", "space"),
        P("tm", "space"),
        P(),
    )
    return jax.shard_map(
        per_device_body,
        mesh=mesh,
        in_specs=placed,
        out_specs=(P("tm", ("space", "hyp")), P("space"), P(None, "space")),
        check_vma=False,
    )
```

```python
import functools

import jax
import jax.numpy as jnp
from jax import lax
from jax.experimental import pallas as pl
from jax.experimental.pallas import tpu as pltpu
from jax.sharding import PartitionSpec as P

BAND = 64
INTERPRET = False


def with_halo(block, axis, width):
    count = lax.axis_size(axis)
    if count == 2:
        place = lax.axis_index(axis)
        send = jnp.where(place == 0, block[-width:], block[:width])
        got = lax.ppermute(send, axis, [(0, 1), (1, 0)])
        low = jnp.where(place == 1, got, jnp.zeros_like(got))
        high = jnp.where(place == 0, got, jnp.zeros_like(got))
    else:
        forward = [(i, i + 1) for i in range(count - 1)]
        backward = [(target, source) for source, target in forward]
        low = lax.ppermute(block[-width:], axis, forward)
        high = lax.ppermute(block[:width], axis, backward)
    return jnp.concatenate([low, block, high])


def chain_kernel(*refs, aligned):
    place_ref, hyper_ref, window_ref, nodes_hbm, offsets_hbm = refs[:5]
    blocks = (len(refs) - 13) // 2
    pieces = refs[5 : 5 + blocks]
    outs = refs[5 + blocks : 5 + 2 * blocks]
    out_ref, piv_ref, slv_ref, data_ref, nodes_ref, offsets_ref, sems, piece_sems = refs[5 + 2 * blocks :]
    _, _, rows, width = data_ref.shape
    first = pl.multiple_of(place_ref[1], 128) if aligned else 0
    node_copy = pltpu.make_async_copy(nodes_hbm.at[:, pl.ds(first, width)], nodes_ref, sems.at[0])
    offsets_copy = pltpu.make_async_copy(
        offsets_hbm.at[:, pl.ds(first, width)], offsets_ref, sems.at[1]
    )
    piece_copies = [
        pltpu.make_async_copy(pieces[shift], data_ref.at[shift], piece_sems.at[shift])
        for shift in range(blocks)
    ]
    node_copy.start()
    offsets_copy.start()
    for copy in piece_copies:
        copy.start()
    node_copy.wait()
    offsets_copy.wait()

    place = place_ref[0]
    window = window_ref[...]
    span = window.shape[1]
    near_off = offsets_ref[...]
    ones = jnp.ones((1, width), jnp.float32)
    nearby = jnp.zeros(near_off.shape, jnp.float32)
    own_kappa = None
    for shift in range(-BAND, BAND + 1):
        moved = pltpu.roll(window, (span - BAND - shift) % span, 1)[:, :width]
        if shift == 0:
            own_kappa = moved
        nearby = jnp.where(near_off == shift, moved, nearby)
    weights = nodes_ref[2:6, :]
    edge_sum = (
        weights[0:1] * nearby[0:1]
        + weights[1:2] * nearby[1:2]
        + weights[2:3] * nearby[2:3]
        + weights[3:4] * nearby[3:4]
    )
    spatial = jnp.exp(2.0 * hyper_ref[0] * ones) * (nodes_ref[0:1, :] * own_kappa + edge_sum)
    scaled = jnp.exp(hyper_ref[1] * ones) * spatial
    persist = jnp.tanh(hyper_ref[2] + nodes_ref[1:2, :])
    ns = jnp.exp(hyper_ref[3] * ones)
    ls2 = (1.0 - persist * persist) / persist
    sp = scaled * (1.0 + persist * persist)
    mps = -persist * scaled
    qs = 2.0 * persist * (1.0 - persist * persist) * scaled
    two_ls2 = 2.0 * ls2
    zeros = jnp.zeros_like(sp)
    carry = (zeros,) * 11
    for copy in piece_copies:
        copy.wait()
    for block in range(blocks):
        slot = lax.rem(place - block + blocks, blocks)

        def forward(t, carry):
            inv, t0, t1, t2, t3, solved, c0, c1, c2, c3, logs = carry
            rough = data_ref[slot, 0, pl.ds(t, 1), :]
            coup = data_ref[slot, 1, pl.ds(t, 1), :]
            weight = data_ref[slot, 2, pl.ds(t, 1), :]
            obs = data_ref[slot, 3, pl.ds(t, 1), :]
            prior = sp * rough
            nugget = ns * weight
            diagonal = prior + nugget
            offdiag = mps * coup
            pivots = diagonal - offdiag * offdiag * inv
            ratios = offdiag * inv
            rr = ratios * ratios
            t0 = rr * t0 + 2.0 * prior - 4.0 * offdiag * ratios
            t1 = rr * t1 + prior - 2.0 * offdiag * ratios
            t2 = rr * t2 + qs * rough - two_ls2 * offdiag * ratios
            t3 = rr * t3 + nugget
            solved = obs - ratios * solved
            inv = 1.0 / pivots
            c0 = c0 + 0.5 * t0 * inv
            c1 = c1 + 0.5 * t1 * inv
            c2 = c2 + 0.5 * t2 * inv
            c3 = c3 + 0.5 * t3 * inv
            logs = logs + jnp.log(pivots)
            piv_ref[block, pl.ds(t, 1), :] = inv
            slv_ref[block, pl.ds(t, 1), :] = solved
            return (inv, t0, t1, t2, t3, solved, c0, c1, c2, c3, logs)

        carry = lax.fori_loop(0, rows, forward, carry, unroll=8)
    c0, c1, c2, c3, logs = carry[6:]
    closing = (zeros,) * 5
    for block in reversed(range(blocks)):
        slot = lax.rem(place - block + blocks, blocks)

        def backward(i, carry):
            t = rows - 1 - i
            following, q0, q1, q2, q3 = carry
            rough = data_ref[slot, 0, pl.ds(t, 1), :]
            coup = data_ref[slot, 1, pl.ds(t, 1), :]
            weight = data_ref[slot, 2, pl.ds(t, 1), :]
            prior = sp * rough
            nugget = ns * weight
            offdiag = mps * coup
            values = (slv_ref[block, pl.ds(t, 1), :] - following) * piv_ref[block, pl.ds(t, 1), :]
            q0 = q0 + 2.0 * prior * values * values + 4.0 * values * following
            q1 = q1 + prior * values * values + 2.0 * values * following
            q2 = q2 + qs * rough * values * values + two_ls2 * values * following
            q3 = q3 + nugget * values * values
            out_ref[block, pl.ds(t, 1), :] = values
            return (offdiag * values, q0, q1, q2, q3)

        closing = lax.fori_loop(0, rows, backward, closing, unroll=8)
    q0, q1, q2, q3 = closing[1:]
    scale = 1.0 / (rows * blocks)
    stats = jnp.concatenate(
        [
            logs * scale,
            (c0 - 0.5 * q0) * scale,
            (c1 - 0.5 * q1) * scale,
            (c2 - 0.5 * q2) * scale,
            (c3 - 0.5 * q3) * scale,
            jnp.zeros((3, width), jnp.float32),
        ],
        axis=0,
    )
    for block in range(blocks):
        out_ref[block, rows : rows + 8, :] = stats
    for shift in range(blocks):
        outs[shift][...] = out_ref[lax.rem(place + shift, blocks)]


def run_chain(place, hyper, window, nodes, offsets, pieces):
    blocks = len(pieces)
    _, rows, width = pieces[0].shape
    vmem = pl.BlockSpec(memory_space=pltpu.VMEM)
    smem = pl.BlockSpec(memory_space=pltpu.SMEM)
    hbm = pl.BlockSpec(memory_space=pl.ANY)
    return pl.pallas_call(
        functools.partial(chain_kernel, aligned=nodes.shape[1] != width),
        out_shape=[jax.ShapeDtypeStruct((rows + 8, width), jnp.float32)] * blocks,
        in_specs=[smem, smem, vmem, hbm, hbm] + [hbm] * blocks,
        out_specs=[vmem] * blocks,
        scratch_shapes=[
            pltpu.VMEM((blocks, rows + 8, width), jnp.float32),
            pltpu.VMEM((blocks, rows, width), jnp.float32),
            pltpu.VMEM((blocks, rows, width), jnp.float32),
            pltpu.VMEM((blocks, 4, rows, width), jnp.float32),
            pltpu.VMEM((6, width), jnp.float32),
            pltpu.VMEM((4, width), jnp.int32),
            pltpu.SemaphoreType.DMA((2,)),
            pltpu.SemaphoreType.DMA((blocks,)),
        ],
        interpret=INTERPRET,
    )(place, hyper, window, nodes, offsets, *pieces)


def place_kernel(place_ref, *refs):
    blocks = len(refs) - 3
    pieces = refs[:blocks]
    sol_ref, stat_ref, sems = refs[blocks:]
    rows = sol_ref.shape[0]
    width = pieces[0].shape[1]
    place = place_ref[0]
    copies = []
    for shift in range(blocks):
        column = pl.multiple_of(lax.rem(place - shift + blocks, blocks) * width, 128)
        copies.append(
            pltpu.make_async_copy(
                pieces[shift].at[0:rows, :], sol_ref.at[:, pl.ds(column, width)], sems.at[0, shift]
            )
        )
        copies.append(
            pltpu.make_async_copy(
                pieces[shift].at[rows : rows + 8, :],
                stat_ref.at[:, pl.ds(column, width)],
                sems.at[1, shift],
            )
        )
    for copy in copies:
        copy.start()
    for copy in copies:
        copy.wait()


def run_place(place, pieces):
    blocks = len(pieces)
    rows = pieces[0].shape[0] - 8
    width = pieces[0].shape[1]
    hbm = pl.BlockSpec(memory_space=pl.ANY)
    smem = pl.BlockSpec(memory_space=pltpu.SMEM)
    return pl.pallas_call(
        place_kernel,
        out_shape=(
            jax.ShapeDtypeStruct((rows, blocks * width), jnp.float32),
            jax.ShapeDtypeStruct((8, blocks * width), jnp.float32),
        ),
        in_specs=[smem] + [hbm] * blocks,
        out_specs=(hbm, hbm),
        scratch_shapes=[pltpu.SemaphoreType.DMA((2, blocks))],
        interpret=INTERPRET,
    )(place, *pieces)


def per_device_body(
    log_kappa,
    node_mass,
    rho_base,
    edge_weight,
    offsets,
    roughness,
    coupling,
    obs_weight,
    observed,
    hyper_params,
):
    row_count, full_width = roughness.shape
    time_count = lax.axis_size("tm")
    hyp_count = lax.axis_size("hyp")
    time_place = lax.axis_index("tm")
    hyp_place = lax.axis_index("hyp")
    quarter = full_width // hyp_count
    chunk = quarter // time_count
    first = hyp_place * quarter + time_place * chunk

    kappa_sq = jnp.exp(2.0 * log_kappa)
    padded = with_halo(kappa_sq, "space", BAND)

    stacked = jnp.stack([roughness, coupling, obs_weight, observed])
    pieces = [
        lax.dynamic_slice_in_dim(
            stacked,
            hyp_place * quarter + lax.rem(time_place + shift, time_count) * chunk,
            chunk,
            axis=2,
        )
        for shift in range(time_count)
    ]
    arrived = [pieces[0]] + [
        lax.ppermute(
            pieces[shift],
            "tm",
            [(i, (i + shift) % time_count) for i in range(time_count)],
        )
        for shift in range(1, time_count)
    ]
    place = jnp.stack([time_place, first]).astype(jnp.int32)
    window = lax.dynamic_slice_in_dim(padded, first, chunk + 2 * BAND)[None]
    nodes = jnp.concatenate([node_mass[None], rho_base[None], edge_weight], axis=0)
    near_off = offsets
    if chunk % 128:
        nodes = lax.dynamic_slice_in_dim(nodes, first, chunk, axis=1)
        near_off = lax.dynamic_slice_in_dim(offsets, first, chunk, axis=1)
    payload = run_chain(place, hyper_params, window, nodes, near_off, arrived)
    returned = [payload[0]] + [
        lax.ppermute(
            payload[shift],
            "tm",
            [(i, (i + shift) % time_count) for i in range(time_count)],
        )
        for shift in range(1, time_count)
    ]
    if chunk % 128 == 0:
        solution_out, stats_out = run_place(place, returned)
        stats_quarter = stats_out[:5]
    else:
        ordered = jnp.take(
            jnp.stack(returned),
            lax.rem(time_place - jnp.arange(time_count) + time_count, time_count),
            axis=0,
        )
        solution_out = ordered[:, :row_count].transpose(1, 0, 2).reshape(row_count, quarter)
        stats_quarter = ordered[:, row_count : row_count + 5].transpose(1, 0, 2).reshape(5, quarter)
    stats_full = lax.all_gather(stats_quarter, "hyp", axis=1, tiled=True)
    return (solution_out, stats_full[0], stats_full[1:5])


def solution(mesh):
    placed = (
        P("space"),
        P("space"),
        P("space"),
        P(None, "space"),
        P(None, "space"),
        P("tm", "space"),
        P("tm", "space"),
        P("tm", "space"),
        P("tm", "space"),
        P(),
    )
    return jax.shard_map(
        per_device_body,
        mesh=mesh,
        in_specs=placed,
        out_specs=(P("tm", ("space", "hyp")), P("space"), P(None, "space")),
        check_vma=False,
    )
```

```python
import functools

import jax
import jax.numpy as jnp
from jax import lax
from jax.experimental import pallas as pl
from jax.experimental.pallas import tpu as pltpu
from jax.sharding import PartitionSpec as P

BAND = 64
INTERPRET = False


def with_halo(block, axis, width):
    count = lax.axis_size(axis)
    if count == 2:
        place = lax.axis_index(axis)
        send = jnp.where(place == 0, block[-width:], block[:width])
        got = lax.ppermute(send, axis, [(0, 1), (1, 0)])
        low = jnp.where(place == 1, got, jnp.zeros_like(got))
        high = jnp.where(place == 0, got, jnp.zeros_like(got))
    else:
        forward = [(i, i + 1) for i in range(count - 1)]
        backward = [(target, source) for source, target in forward]
        low = lax.ppermute(block[-width:], axis, forward)
        high = lax.ppermute(block[:width], axis, backward)
    return jnp.concatenate([low, block, high])


def chain_kernel(*refs, aligned):
    place_ref, hyper_ref, window_ref, nodes_hbm, offsets_hbm = refs[:5]
    blocks = (len(refs) - 13) // 2
    pieces = refs[5 : 5 + blocks]
    outs = refs[5 + blocks : 5 + 2 * blocks]
    out_ref, piv_ref, slv_ref, data_ref, nodes_ref, offsets_ref, sems, piece_sems = refs[5 + 2 * blocks :]
    _, _, rows, width = data_ref.shape
    first = pl.multiple_of(place_ref[1], 128) if aligned else 0
    node_copy = pltpu.make_async_copy(nodes_hbm.at[:, pl.ds(first, width)], nodes_ref, sems.at[0])
    offsets_copy = pltpu.make_async_copy(
        offsets_hbm.at[:, pl.ds(first, width)], offsets_ref, sems.at[1]
    )
    piece_copies = [
        pltpu.make_async_copy(pieces[shift], data_ref.at[shift], piece_sems.at[shift])
        for shift in range(blocks)
    ]
    node_copy.start()
    offsets_copy.start()
    for copy in piece_copies:
        copy.start()
    node_copy.wait()
    offsets_copy.wait()

    place = place_ref[0]
    window = window_ref[...]
    span = window.shape[1]
    near_off = offsets_ref[...]
    ones = jnp.ones((1, width), jnp.float32)
    nearby = jnp.zeros(near_off.shape, jnp.float32)
    own_kappa = None
    for shift in range(-BAND, BAND + 1):
        moved = pltpu.roll(window, (span - BAND - shift) % span, 1)[:, :width]
        if shift == 0:
            own_kappa = moved
        nearby = jnp.where(near_off == shift, moved, nearby)
    weights = nodes_ref[2:6, :]
    edge_sum = (
        weights[0:1] * nearby[0:1]
        + weights[1:2] * nearby[1:2]
        + weights[2:3] * nearby[2:3]
        + weights[3:4] * nearby[3:4]
    )
    spatial = jnp.exp(2.0 * hyper_ref[0] * ones) * (nodes_ref[0:1, :] * own_kappa + edge_sum)
    scaled = jnp.exp(hyper_ref[1] * ones) * spatial
    persist = jnp.tanh(hyper_ref[2] + nodes_ref[1:2, :])
    ns = jnp.exp(hyper_ref[3] * ones)
    ls2 = (1.0 - persist * persist) / persist
    sp = scaled * (1.0 + persist * persist)
    mps = -persist * scaled
    qs = 2.0 * persist * (1.0 - persist * persist) * scaled
    two_ls2 = 2.0 * ls2
    zeros = jnp.zeros_like(sp)
    carry = (zeros,) * 11
    for copy in piece_copies:
        copy.wait()
    for block in range(blocks):
        slot = lax.rem(place - block + blocks, blocks)

        def forward(t, carry):
            inv, t0, t1, t2, t3, solved, c0, c1, c2, c3, logs = carry
            rough = data_ref[slot, 0, pl.ds(t, 1), :]
            coup = data_ref[slot, 1, pl.ds(t, 1), :]
            weight = data_ref[slot, 2, pl.ds(t, 1), :]
            obs = data_ref[slot, 3, pl.ds(t, 1), :]
            prior = sp * rough
            nugget = ns * weight
            diagonal = prior + nugget
            offdiag = mps * coup
            pivots = diagonal - offdiag * offdiag * inv
            ratios = offdiag * inv
            rr = ratios * ratios
            t0 = rr * t0 + 2.0 * prior - 4.0 * offdiag * ratios
            t1 = rr * t1 + prior - 2.0 * offdiag * ratios
            t2 = rr * t2 + qs * rough - two_ls2 * offdiag * ratios
            t3 = rr * t3 + nugget
            solved = obs - ratios * solved
            inv = 1.0 / pivots
            c0 = c0 + 0.5 * t0 * inv
            c1 = c1 + 0.5 * t1 * inv
            c2 = c2 + 0.5 * t2 * inv
            c3 = c3 + 0.5 * t3 * inv
            logs = logs + jnp.log(pivots)
            piv_ref[block, pl.ds(t, 1), :] = inv
            slv_ref[block, pl.ds(t, 1), :] = solved
            return (inv, t0, t1, t2, t3, solved, c0, c1, c2, c3, logs)

        carry = lax.fori_loop(0, rows, forward, carry, unroll=8)
    c0, c1, c2, c3, logs = carry[6:]
    closing = (zeros,) * 5
    for block in reversed(range(blocks)):
        slot = lax.rem(place - block + blocks, blocks)

        def backward(i, carry):
            t = rows - 1 - i
            following, q0, q1, q2, q3 = carry
            rough = data_ref[slot, 0, pl.ds(t, 1), :]
            coup = data_ref[slot, 1, pl.ds(t, 1), :]
            weight = data_ref[slot, 2, pl.ds(t, 1), :]
            prior = sp * rough
            nugget = ns * weight
            offdiag = mps * coup
            values = (slv_ref[block, pl.ds(t, 1), :] - following) * piv_ref[block, pl.ds(t, 1), :]
            q0 = q0 + 2.0 * prior * values * values + 4.0 * values * following
            q1 = q1 + prior * values * values + 2.0 * values * following
            q2 = q2 + qs * rough * values * values + two_ls2 * values * following
            q3 = q3 + nugget * values * values
            out_ref[block, pl.ds(t, 1), :] = values
            return (offdiag * values, q0, q1, q2, q3)

        closing = lax.fori_loop(0, rows, backward, closing, unroll=8)
    q0, q1, q2, q3 = closing[1:]
    scale = 1.0 / (rows * blocks)
    stats = jnp.concatenate(
        [
            logs * scale,
            (c0 - 0.5 * q0) * scale,
            (c1 - 0.5 * q1) * scale,
            (c2 - 0.5 * q2) * scale,
            (c3 - 0.5 * q3) * scale,
            jnp.zeros((3, width), jnp.float32),
        ],
        axis=0,
    )
    for block in range(blocks):
        out_ref[block, rows : rows + 8, :] = stats
    for shift in range(blocks):
        outs[shift][...] = out_ref[lax.rem(place + shift, blocks)]


def run_chain(place, hyper, window, nodes, offsets, pieces):
    blocks = len(pieces)
    _, rows, width = pieces[0].shape
    vmem = pl.BlockSpec(memory_space=pltpu.VMEM)
    smem = pl.BlockSpec(memory_space=pltpu.SMEM)
    hbm = pl.BlockSpec(memory_space=pltpu.HBM)
    return pl.pallas_call(
        functools.partial(chain_kernel, aligned=nodes.shape[1] != width),
        out_shape=[jax.ShapeDtypeStruct((rows + 8, width), jnp.float32)] * blocks,
        in_specs=[smem, smem, vmem, hbm, hbm] + [hbm] * blocks,
        out_specs=[vmem] * blocks,
        scratch_shapes=[
            pltpu.VMEM((blocks, rows + 8, width), jnp.float32),
            pltpu.VMEM((blocks, rows, width), jnp.float32),
            pltpu.VMEM((blocks, rows, width), jnp.float32),
            pltpu.VMEM((blocks, 4, rows, width), jnp.float32),
            pltpu.VMEM((6, width), jnp.float32),
            pltpu.VMEM((4, width), jnp.int32),
            pltpu.SemaphoreType.DMA((2,)),
            pltpu.SemaphoreType.DMA((blocks,)),
        ],
        interpret=INTERPRET,
    )(place, hyper, window, nodes, offsets, *pieces)


def place_kernel(place_ref, *refs):
    blocks = len(refs) - 4
    pieces = refs[:blocks]
    sol_ref, stat_ref, arrived_ref, sems = refs[blocks:]
    rows = sol_ref.shape[0]
    width = pieces[0].shape[1]
    place = place_ref[0]
    copies = [
        pltpu.make_async_copy(pieces[shift], arrived_ref.at[shift - 1], sems.at[shift - 1])
        for shift in range(1, blocks)
    ]
    for copy in copies:
        copy.start()
    for shift in range(blocks):
        column = pl.multiple_of(lax.rem(place - shift + blocks, blocks) * width, 128)
        if shift == 0:
            piece = pieces[0][...]
        else:
            copies[shift - 1].wait()
            piece = arrived_ref[shift - 1]
        sol_ref[:, pl.ds(column, width)] = piece[0:rows, :]
        stat_ref[:, pl.ds(column, width)] = piece[rows : rows + 8, :]


def run_place(place, pieces):
    blocks = len(pieces)
    rows = pieces[0].shape[0] - 8
    width = pieces[0].shape[1]
    vmem = pl.BlockSpec(memory_space=pltpu.VMEM)
    smem = pl.BlockSpec(memory_space=pltpu.SMEM)
    hbm = pl.BlockSpec(memory_space=pltpu.HBM)
    return pl.pallas_call(
        place_kernel,
        out_shape=(
            jax.ShapeDtypeStruct((rows, blocks * width), jnp.float32),
            jax.ShapeDtypeStruct((8, blocks * width), jnp.float32),
        ),
        in_specs=[smem, vmem] + [hbm] * (blocks - 1),
        out_specs=(vmem, vmem),
        scratch_shapes=[
            pltpu.VMEM((blocks - 1, rows + 8, width), jnp.float32),
            pltpu.SemaphoreType.DMA((blocks - 1,)),
        ],
        interpret=INTERPRET,
    )(place, *pieces)


def per_device_body(
    log_kappa,
    node_mass,
    rho_base,
    edge_weight,
    offsets,
    roughness,
    coupling,
    obs_weight,
    observed,
    hyper_params,
):
    row_count, full_width = roughness.shape
    time_count = lax.axis_size("tm")
    hyp_count = lax.axis_size("hyp")
    time_place = lax.axis_index("tm")
    hyp_place = lax.axis_index("hyp")
    quarter = full_width // hyp_count
    chunk = quarter // time_count
    first = hyp_place * quarter + time_place * chunk

    kappa_sq = jnp.exp(2.0 * log_kappa)
    padded = with_halo(kappa_sq, "space", BAND)

    pieces = []
    for shift in range(time_count):
        start = hyp_place * quarter + lax.rem(time_place + shift, time_count) * chunk
        pieces.append(
            jnp.stack(
                [
                    lax.dynamic_slice_in_dim(rows, start, chunk, axis=1)
                    for rows in (roughness, coupling, obs_weight, observed)
                ]
            )
        )
    arrived = [pieces[0]] + [
        lax.ppermute(
            pieces[shift],
            "tm",
            [(i, (i + shift) % time_count) for i in range(time_count)],
        )
        for shift in range(1, time_count)
    ]
    place = jnp.stack([time_place, first]).astype(jnp.int32)
    window = lax.dynamic_slice_in_dim(padded, first, chunk + 2 * BAND)[None]
    nodes = jnp.concatenate([node_mass[None], rho_base[None], edge_weight], axis=0)
    near_off = offsets
    if chunk % 128:
        nodes = lax.dynamic_slice_in_dim(nodes, first, chunk, axis=1)
        near_off = lax.dynamic_slice_in_dim(offsets, first, chunk, axis=1)
    payload = run_chain(place, hyper_params, window, nodes, near_off, arrived)
    returned = [payload[0]] + [
        lax.ppermute(
            payload[shift],
            "tm",
            [(i, (i + shift) % time_count) for i in range(time_count)],
        )
        for shift in range(1, time_count)
    ]
    if chunk % 128 == 0:
        solution_out, stats_out = run_place(place, returned)
        stats_quarter = stats_out[:5]
    else:
        ordered = jnp.take(
            jnp.stack(returned),
            lax.rem(time_place - jnp.arange(time_count) + time_count, time_count),
            axis=0,
        )
        solution_out = ordered[:, :row_count].transpose(1, 0, 2).reshape(row_count, quarter)
        stats_quarter = ordered[:, row_count : row_count + 5].transpose(1, 0, 2).reshape(5, quarter)
    stats_full = lax.all_gather(stats_quarter, "hyp", axis=1, tiled=True)
    return (solution_out, stats_full[0], stats_full[1:5])


def solution(mesh):
    placed = (
        P("space"),
        P("space"),
        P("space"),
        P(None, "space"),
        P(None, "space"),
        P("tm", "space"),
        P("tm", "space"),
        P("tm", "space"),
        P("tm", "space"),
        P(),
    )
    return jax.shard_map(
        per_device_body,
        mesh=mesh,
        in_specs=placed,
        out_specs=(P("tm", ("space", "hyp")), P("space"), P(None, "space")),
        check_vma=False,
    )
```

```python
import functools

import jax
import jax.numpy as jnp
from jax import lax
from jax.experimental import pallas as pl
from jax.experimental.pallas import tpu as pltpu
from jax.sharding import PartitionSpec as P

BAND = 64
INTERPRET = False


def with_halo(block, axis, width):
    count = lax.axis_size(axis)
    if count == 2:
        place = lax.axis_index(axis)
        send = jnp.where(place == 0, block[-width:], block[:width])
        got = lax.ppermute(send, axis, [(0, 1), (1, 0)])
        low = jnp.where(place == 1, got, jnp.zeros_like(got))
        high = jnp.where(place == 0, got, jnp.zeros_like(got))
    else:
        forward = [(i, i + 1) for i in range(count - 1)]
        backward = [(target, source) for source, target in forward]
        low = lax.ppermute(block[-width:], axis, forward)
        high = lax.ppermute(block[:width], axis, backward)
    return jnp.concatenate([low, block, high])


def chain_kernel(*refs, aligned):
    place_ref, hyper_ref, window_ref, nodes_hbm, offsets_hbm = refs[:5]
    blocks = (len(refs) - 13) // 2
    pieces = refs[5 : 5 + blocks]
    outs = refs[5 + blocks : 5 + 2 * blocks]
    out_ref, piv_ref, slv_ref, data_ref, nodes_ref, offsets_ref, sems, piece_sems = refs[5 + 2 * blocks :]
    _, _, rows, width = data_ref.shape
    first = pl.multiple_of(place_ref[1], 128) if aligned else 0
    node_copy = pltpu.make_async_copy(nodes_hbm.at[:, pl.ds(first, width)], nodes_ref, sems.at[0])
    offsets_copy = pltpu.make_async_copy(
        offsets_hbm.at[:, pl.ds(first, width)], offsets_ref, sems.at[1]
    )
    piece_copies = [
        pltpu.make_async_copy(pieces[shift], data_ref.at[shift], piece_sems.at[shift])
        for shift in range(blocks)
    ]
    node_copy.start()
    offsets_copy.start()
    for copy in piece_copies:
        copy.start()
    node_copy.wait()
    offsets_copy.wait()

    place = place_ref[0]
    window = window_ref[...]
    span = window.shape[1]
    near_off = offsets_ref[...]
    ones = jnp.ones((1, width), jnp.float32)
    nearby = jnp.zeros(near_off.shape, jnp.float32)
    own_kappa = None
    for shift in range(-BAND, BAND + 1):
        moved = pltpu.roll(window, (span - BAND - shift) % span, 1)[:, :width]
        if shift == 0:
            own_kappa = moved
        nearby = jnp.where(near_off == shift, moved, nearby)
    weights = nodes_ref[2:6, :]
    edge_sum = (
        weights[0:1] * nearby[0:1]
        + weights[1:2] * nearby[1:2]
        + weights[2:3] * nearby[2:3]
        + weights[3:4] * nearby[3:4]
    )
    spatial = jnp.exp(2.0 * hyper_ref[0] * ones) * (nodes_ref[0:1, :] * own_kappa + edge_sum)
    scaled = jnp.exp(hyper_ref[1] * ones) * spatial
    persist = jnp.tanh(hyper_ref[2] + nodes_ref[1:2, :])
    ns = jnp.exp(hyper_ref[3] * ones)
    ls2 = (1.0 - persist * persist) / persist
    sp = scaled * (1.0 + persist * persist)
    mps = -persist * scaled
    qs = 2.0 * persist * (1.0 - persist * persist) * scaled
    two_ls2 = 2.0 * ls2
    zeros = jnp.zeros_like(sp)
    carry = (zeros,) * 11
    for copy in piece_copies:
        copy.wait()
    for block in range(blocks):
        slot = lax.rem(place - block + blocks, blocks)

        def forward(t, carry):
            inv, t0, t1, t2, t3, solved, c0, c1, c2, c3, logs = carry
            rough = data_ref[slot, 0, pl.ds(t, 1), :]
            coup = data_ref[slot, 1, pl.ds(t, 1), :]
            weight = data_ref[slot, 2, pl.ds(t, 1), :]
            obs = data_ref[slot, 3, pl.ds(t, 1), :]
            prior = sp * rough
            nugget = ns * weight
            diagonal = prior + nugget
            offdiag = mps * coup
            pivots = diagonal - offdiag * offdiag * inv
            ratios = offdiag * inv
            rr = ratios * ratios
            t0 = rr * t0 + 2.0 * prior - 4.0 * offdiag * ratios
            t1 = rr * t1 + prior - 2.0 * offdiag * ratios
            t2 = rr * t2 + qs * rough - two_ls2 * offdiag * ratios
            t3 = rr * t3 + nugget
            solved = obs - ratios * solved
            inv = 1.0 / pivots
            c0 = c0 + 0.5 * t0 * inv
            c1 = c1 + 0.5 * t1 * inv
            c2 = c2 + 0.5 * t2 * inv
            c3 = c3 + 0.5 * t3 * inv
            logs = logs + jnp.log(pivots)
            piv_ref[block, pl.ds(t, 1), :] = inv
            slv_ref[block, pl.ds(t, 1), :] = solved
            return (inv, t0, t1, t2, t3, solved, c0, c1, c2, c3, logs)

        carry = lax.fori_loop(0, rows, forward, carry, unroll=True)
    c0, c1, c2, c3, logs = carry[6:]
    closing = (zeros,) * 5
    for block in reversed(range(blocks)):
        slot = lax.rem(place - block + blocks, blocks)

        def backward(i, carry):
            t = rows - 1 - i
            following, q0, q1, q2, q3 = carry
            rough = data_ref[slot, 0, pl.ds(t, 1), :]
            coup = data_ref[slot, 1, pl.ds(t, 1), :]
            weight = data_ref[slot, 2, pl.ds(t, 1), :]
            prior = sp * rough
            nugget = ns * weight
            offdiag = mps * coup
            values = (slv_ref[block, pl.ds(t, 1), :] - following) * piv_ref[block, pl.ds(t, 1), :]
            q0 = q0 + 2.0 * prior * values * values + 4.0 * values * following
            q1 = q1 + prior * values * values + 2.0 * values * following
            q2 = q2 + qs * rough * values * values + two_ls2 * values * following
            q3 = q3 + nugget * values * values
            out_ref[block, pl.ds(t, 1), :] = values
            return (offdiag * values, q0, q1, q2, q3)

        closing = lax.fori_loop(0, rows, backward, closing, unroll=True)
    q0, q1, q2, q3 = closing[1:]
    scale = 1.0 / (rows * blocks)
    stats = jnp.concatenate(
        [
            logs * scale,
            (c0 - 0.5 * q0) * scale,
            (c1 - 0.5 * q1) * scale,
            (c2 - 0.5 * q2) * scale,
            (c3 - 0.5 * q3) * scale,
            jnp.zeros((3, width), jnp.float32),
        ],
        axis=0,
    )
    for block in range(blocks):
        out_ref[block, rows : rows + 8, :] = stats
    for shift in range(blocks):
        outs[shift][...] = out_ref[lax.rem(place + shift, blocks)]


def run_chain(place, hyper, window, nodes, offsets, pieces):
    blocks = len(pieces)
    _, rows, width = pieces[0].shape
    vmem = pl.BlockSpec(memory_space=pltpu.VMEM)
    smem = pl.BlockSpec(memory_space=pltpu.SMEM)
    hbm = pl.BlockSpec(memory_space=pl.ANY)
    return pl.pallas_call(
        functools.partial(chain_kernel, aligned=nodes.shape[1] != width),
        out_shape=[jax.ShapeDtypeStruct((rows + 8, width), jnp.float32)] * blocks,
        in_specs=[smem, smem, vmem, hbm, hbm] + [hbm] * blocks,
        out_specs=[vmem] * blocks,
        scratch_shapes=[
            pltpu.VMEM((blocks, rows + 8, width), jnp.float32),
            pltpu.VMEM((blocks, rows, width), jnp.float32),
            pltpu.VMEM((blocks, rows, width), jnp.float32),
            pltpu.VMEM((blocks, 4, rows, width), jnp.float32),
            pltpu.VMEM((6, width), jnp.float32),
            pltpu.VMEM((4, width), jnp.int32),
            pltpu.SemaphoreType.DMA((2,)),
            pltpu.SemaphoreType.DMA((blocks,)),
        ],
        interpret=INTERPRET,
    )(place, hyper, window, nodes, offsets, *pieces)


def place_kernel(place_ref, *refs):
    blocks = len(refs) - 2
    pieces = refs[:blocks]
    sol_ref, stat_ref = refs[blocks:]
    rows = sol_ref.shape[0]
    width = pieces[0].shape[1]
    place = place_ref[0]
    for shift in range(blocks):
        column = pl.multiple_of(lax.rem(place - shift + blocks, blocks) * width, 128)
        sol_ref[:, pl.ds(column, width)] = pieces[shift][0:rows, :]
        stat_ref[:, pl.ds(column, width)] = pieces[shift][rows : rows + 8, :]


def run_place(place, pieces):
    blocks = len(pieces)
    rows = pieces[0].shape[0] - 8
    width = pieces[0].shape[1]
    vmem = pl.BlockSpec(memory_space=pltpu.VMEM)
    smem = pl.BlockSpec(memory_space=pltpu.SMEM)
    return pl.pallas_call(
        place_kernel,
        out_shape=(
            jax.ShapeDtypeStruct((rows, blocks * width), jnp.float32),
            jax.ShapeDtypeStruct((8, blocks * width), jnp.float32),
        ),
        in_specs=[smem] + [vmem] * blocks,
        out_specs=(vmem, vmem),
        interpret=INTERPRET,
    )(place, *pieces)


def per_device_body(
    log_kappa,
    node_mass,
    rho_base,
    edge_weight,
    offsets,
    roughness,
    coupling,
    obs_weight,
    observed,
    hyper_params,
):
    row_count, full_width = roughness.shape
    time_count = lax.axis_size("tm")
    hyp_count = lax.axis_size("hyp")
    time_place = lax.axis_index("tm")
    hyp_place = lax.axis_index("hyp")
    quarter = full_width // hyp_count
    chunk = quarter // time_count
    first = hyp_place * quarter + time_place * chunk

    kappa_sq = jnp.exp(2.0 * log_kappa)
    padded = with_halo(kappa_sq, "space", BAND)

    stacked = jnp.stack([roughness, coupling, obs_weight, observed])
    pieces = [
        lax.dynamic_slice_in_dim(
            stacked,
            hyp_place * quarter + lax.rem(time_place + shift, time_count) * chunk,
            chunk,
            axis=2,
        )
        for shift in range(time_count)
    ]
    arrived = [pieces[0]] + [
        lax.ppermute(
            pieces[shift],
            "tm",
            [(i, (i + shift) % time_count) for i in range(time_count)],
        )
        for shift in range(1, time_count)
    ]
    place = jnp.stack([time_place, first]).astype(jnp.int32)
    window = lax.dynamic_slice_in_dim(padded, first, chunk + 2 * BAND)[None]
    nodes = jnp.concatenate([node_mass[None], rho_base[None], edge_weight], axis=0)
    near_off = offsets
    if chunk % 128:
        nodes = lax.dynamic_slice_in_dim(nodes, first, chunk, axis=1)
        near_off = lax.dynamic_slice_in_dim(offsets, first, chunk, axis=1)
    payload = run_chain(place, hyper_params, window, nodes, near_off, arrived)
    returned = [payload[0]] + [
        lax.ppermute(
            payload[shift],
            "tm",
            [(i, (i + shift) % time_count) for i in range(time_count)],
        )
        for shift in range(1, time_count)
    ]
    if chunk % 128 == 0:
        solution_out, stats_out = run_place(place, returned)
        stats_quarter = stats_out[:5]
    else:
        ordered = jnp.take(
            jnp.stack(returned),
            lax.rem(time_place - jnp.arange(time_count) + time_count, time_count),
            axis=0,
        )
        solution_out = ordered[:, :row_count].transpose(1, 0, 2).reshape(row_count, quarter)
        stats_quarter = ordered[:, row_count : row_count + 5].transpose(1, 0, 2).reshape(5, quarter)
    stats_full = lax.all_gather(stats_quarter, "hyp", axis=1, tiled=True)
    return (solution_out, stats_full[0], stats_full[1:5])


def solution(mesh):
    placed = (
        P("space"),
        P("space"),
        P("space"),
        P(None, "space"),
        P(None, "space"),
        P("tm", "space"),
        P("tm", "space"),
        P("tm", "space"),
        P("tm", "space"),
        P(),
    )
    return jax.shard_map(
        per_device_body,
        mesh=mesh,
        in_specs=placed,
        out_specs=(P("tm", ("space", "hyp")), P("space"), P(None, "space")),
        check_vma=False,
    )
```

```python
import functools

import jax
import jax.numpy as jnp
from jax import lax
from jax.experimental import pallas as pl
from jax.experimental.pallas import tpu as pltpu
from jax.sharding import PartitionSpec as P

BAND = 64
INTERPRET = False


def with_halo(block, axis, width):
    count = lax.axis_size(axis)
    if count == 2:
        place = lax.axis_index(axis)
        send = jnp.where(place == 0, block[-width:], block[:width])
        got = lax.ppermute(send, axis, [(0, 1), (1, 0)])
        low = jnp.where(place == 1, got, jnp.zeros_like(got))
        high = jnp.where(place == 0, got, jnp.zeros_like(got))
    else:
        forward = [(i, i + 1) for i in range(count - 1)]
        backward = [(target, source) for source, target in forward]
        low = lax.ppermute(block[-width:], axis, forward)
        high = lax.ppermute(block[:width], axis, backward)
    return jnp.concatenate([low, block, high])


def param_kernel(place_ref, hyper_ref, window_ref, nodes_hbm, offsets_hbm, par_ref, nodes_ref, offsets_ref, sems, *, aligned):
    width = par_ref.shape[1]
    first = pl.multiple_of(place_ref[1], 128) if aligned else 0
    node_copy = pltpu.make_async_copy(nodes_hbm.at[:, pl.ds(first, width)], nodes_ref, sems.at[0])
    offsets_copy = pltpu.make_async_copy(
        offsets_hbm.at[:, pl.ds(first, width)], offsets_ref, sems.at[1]
    )
    node_copy.start()
    offsets_copy.start()
    node_copy.wait()
    offsets_copy.wait()
    window = window_ref[...]
    span = window.shape[1]
    near_off = offsets_ref[...]
    ones = jnp.ones((1, width), jnp.float32)
    nearby = jnp.zeros(near_off.shape, jnp.float32)
    own_kappa = None
    for shift in range(-BAND, BAND + 1):
        moved = pltpu.roll(window, (span - BAND - shift) % span, 1)[:, :width]
        if shift == 0:
            own_kappa = moved
        nearby = jnp.where(near_off == shift, moved, nearby)
    weights = nodes_ref[2:6, :]
    edge_sum = (
        weights[0:1] * nearby[0:1]
        + weights[1:2] * nearby[1:2]
        + weights[2:3] * nearby[2:3]
        + weights[3:4] * nearby[3:4]
    )
    spatial = jnp.exp(2.0 * hyper_ref[0] * ones) * (nodes_ref[0:1, :] * own_kappa + edge_sum)
    scaled = jnp.exp(hyper_ref[1] * ones) * spatial
    persist = jnp.tanh(hyper_ref[2] + nodes_ref[1:2, :])
    ns = jnp.exp(hyper_ref[3] * ones)
    ls2 = (1.0 - persist * persist) / persist
    sp = scaled * (1.0 + persist * persist)
    mps = -persist * scaled
    qs = 2.0 * persist * (1.0 - persist * persist) * scaled
    two_ls2 = 2.0 * ls2
    par_ref[0:1, :] = sp
    par_ref[1:2, :] = mps
    par_ref[2:3, :] = qs
    par_ref[3:4, :] = ns
    par_ref[4:5, :] = two_ls2
    par_ref[5:8, :] = jnp.zeros((3, width), jnp.float32)


def run_params(place, hyper, window, nodes, offsets, width):
    vmem = pl.BlockSpec(memory_space=pltpu.VMEM)
    smem = pl.BlockSpec(memory_space=pltpu.SMEM)
    hbm = pl.BlockSpec(memory_space=pl.ANY)
    return pl.pallas_call(
        functools.partial(param_kernel, aligned=nodes.shape[1] != width),
        out_shape=jax.ShapeDtypeStruct((8, width), jnp.float32),
        in_specs=[smem, smem, vmem, hbm, hbm],
        out_specs=vmem,
        scratch_shapes=[
            pltpu.VMEM((6, width), jnp.float32),
            pltpu.VMEM((4, width), jnp.int32),
            pltpu.SemaphoreType.DMA((2,)),
        ],
        interpret=INTERPRET,
    )(place, hyper, window, nodes, offsets)


def chain_kernel(*refs):
    place_ref, par_ref = refs[:2]
    blocks = (len(refs) - 7) // 2
    pieces = refs[2 : 2 + blocks]
    outs = refs[2 + blocks : 2 + 2 * blocks]
    out_ref, piv_ref, slv_ref, data_ref, piece_sems = refs[2 + 2 * blocks :]
    _, _, rows, width = data_ref.shape
    place = place_ref[0]
    piece_copies = [
        pltpu.make_async_copy(pieces[shift], data_ref.at[shift], piece_sems.at[shift])
        for shift in range(blocks)
    ]
    for copy in piece_copies:
        copy.start()
    sp = par_ref[0:1, :]
    mps = par_ref[1:2, :]
    qs = par_ref[2:3, :]
    ns = par_ref[3:4, :]
    two_ls2 = par_ref[4:5, :]
    zeros = jnp.zeros_like(sp)
    carry = (zeros,) * 11
    for copy in piece_copies:
        copy.wait()
    for block in range(blocks):
        slot = lax.rem(place - block + blocks, blocks)

        def forward(t, carry):
            inv, t0, t1, t2, t3, solved, c0, c1, c2, c3, logs = carry
            rough = data_ref[slot, 0, pl.ds(t, 1), :]
            coup = data_ref[slot, 1, pl.ds(t, 1), :]
            weight = data_ref[slot, 2, pl.ds(t, 1), :]
            obs = data_ref[slot, 3, pl.ds(t, 1), :]
            prior = sp * rough
            nugget = ns * weight
            diagonal = prior + nugget
            offdiag = mps * coup
            pivots = diagonal - offdiag * offdiag * inv
            ratios = offdiag * inv
            rr = ratios * ratios
            t0 = rr * t0 + 2.0 * prior - 4.0 * offdiag * ratios
            t1 = rr * t1 + prior - 2.0 * offdiag * ratios
            t2 = rr * t2 + qs * rough - two_ls2 * offdiag * ratios
            t3 = rr * t3 + nugget
            solved = obs - ratios * solved
            inv = 1.0 / pivots
            c0 = c0 + 0.5 * t0 * inv
            c1 = c1 + 0.5 * t1 * inv
            c2 = c2 + 0.5 * t2 * inv
            c3 = c3 + 0.5 * t3 * inv
            logs = logs + jnp.log(pivots)
            piv_ref[block, pl.ds(t, 1), :] = inv
            slv_ref[block, pl.ds(t, 1), :] = solved
            return (inv, t0, t1, t2, t3, solved, c0, c1, c2, c3, logs)

        carry = lax.fori_loop(0, rows, forward, carry, unroll=True)
    c0, c1, c2, c3, logs = carry[6:]
    closing = (zeros,) * 5
    for block in reversed(range(blocks)):
        slot = lax.rem(place - block + blocks, blocks)

        def backward(i, carry):
            t = rows - 1 - i
            following, q0, q1, q2, q3 = carry
            rough = data_ref[slot, 0, pl.ds(t, 1), :]
            coup = data_ref[slot, 1, pl.ds(t, 1), :]
            weight = data_ref[slot, 2, pl.ds(t, 1), :]
            prior = sp * rough
            nugget = ns * weight
            offdiag = mps * coup
            values = (slv_ref[block, pl.ds(t, 1), :] - following) * piv_ref[block, pl.ds(t, 1), :]
            q0 = q0 + 2.0 * prior * values * values + 4.0 * values * following
            q1 = q1 + prior * values * values + 2.0 * values * following
            q2 = q2 + qs * rough * values * values + two_ls2 * values * following
            q3 = q3 + nugget * values * values
            out_ref[block, pl.ds(t, 1), :] = values
            return (offdiag * values, q0, q1, q2, q3)

        closing = lax.fori_loop(0, rows, backward, closing, unroll=True)
    q0, q1, q2, q3 = closing[1:]
    scale = 1.0 / (rows * blocks)
    stats = jnp.concatenate(
        [
            logs * scale,
            (c0 - 0.5 * q0) * scale,
            (c1 - 0.5 * q1) * scale,
            (c2 - 0.5 * q2) * scale,
            (c3 - 0.5 * q3) * scale,
            jnp.zeros((3, width), jnp.float32),
        ],
        axis=0,
    )
    for block in range(blocks):
        out_ref[block, rows : rows + 8, :] = stats
    for shift in range(blocks):
        outs[shift][...] = out_ref[lax.rem(place + shift, blocks)]


def run_chain(place, params, pieces):
    blocks = len(pieces)
    _, rows, width = pieces[0].shape
    vmem = pl.BlockSpec(memory_space=pltpu.VMEM)
    smem = pl.BlockSpec(memory_space=pltpu.SMEM)
    hbm = pl.BlockSpec(memory_space=pl.ANY)
    return pl.pallas_call(
        chain_kernel,
        out_shape=[jax.ShapeDtypeStruct((rows + 8, width), jnp.float32)] * blocks,
        in_specs=[smem, vmem] + [hbm] * blocks,
        out_specs=[vmem] * blocks,
        scratch_shapes=[
            pltpu.VMEM((blocks, rows + 8, width), jnp.float32),
            pltpu.VMEM((blocks, rows, width), jnp.float32),
            pltpu.VMEM((blocks, rows, width), jnp.float32),
            pltpu.VMEM((blocks, 4, rows, width), jnp.float32),
            pltpu.SemaphoreType.DMA((blocks,)),
        ],
        interpret=INTERPRET,
    )(place, params, *pieces)


def place_kernel(place_ref, *refs):
    blocks = len(refs) - 2
    pieces = refs[:blocks]
    sol_ref, stat_ref = refs[blocks:]
    rows = sol_ref.shape[0]
    width = pieces[0].shape[1]
    place = place_ref[0]
    for shift in range(blocks):
        column = pl.multiple_of(lax.rem(place - shift + blocks, blocks) * width, 128)
        sol_ref[:, pl.ds(column, width)] = pieces[shift][0:rows, :]
        stat_ref[:, pl.ds(column, width)] = pieces[shift][rows : rows + 8, :]


def run_place(place, pieces):
    blocks = len(pieces)
    rows = pieces[0].shape[0] - 8
    width = pieces[0].shape[1]
    vmem = pl.BlockSpec(memory_space=pltpu.VMEM)
    smem = pl.BlockSpec(memory_space=pltpu.SMEM)
    return pl.pallas_call(
        place_kernel,
        out_shape=(
            jax.ShapeDtypeStruct((rows, blocks * width), jnp.float32),
            jax.ShapeDtypeStruct((8, blocks * width), jnp.float32),
        ),
        in_specs=[smem] + [vmem] * blocks,
        out_specs=(vmem, vmem),
        interpret=INTERPRET,
    )(place, *pieces)


def per_device_body(
    log_kappa,
    node_mass,
    rho_base,
    edge_weight,
    offsets,
    roughness,
    coupling,
    obs_weight,
    observed,
    hyper_params,
):
    row_count, full_width = roughness.shape
    time_count = lax.axis_size("tm")
    hyp_count = lax.axis_size("hyp")
    time_place = lax.axis_index("tm")
    hyp_place = lax.axis_index("hyp")
    quarter = full_width // hyp_count
    chunk = quarter // time_count
    first = hyp_place * quarter + time_place * chunk

    kappa_sq = jnp.exp(2.0 * log_kappa)
    padded = with_halo(kappa_sq, "space", BAND)

    stacked = jnp.stack([roughness, coupling, obs_weight, observed])
    pieces = [
        lax.dynamic_slice_in_dim(
            stacked,
            hyp_place * quarter + lax.rem(time_place + shift, time_count) * chunk,
            chunk,
            axis=2,
        )
        for shift in range(time_count)
    ]
    arrived = [pieces[0]] + [
        lax.ppermute(
            pieces[shift],
            "tm",
            [(i, (i + shift) % time_count) for i in range(time_count)],
        )
        for shift in range(1, time_count)
    ]
    place = jnp.stack([time_place, first]).astype(jnp.int32)
    window = lax.dynamic_slice_in_dim(padded, first, chunk + 2 * BAND)[None]
    nodes = jnp.concatenate([node_mass[None], rho_base[None], edge_weight], axis=0)
    near_off = offsets
    if chunk % 128:
        nodes = lax.dynamic_slice_in_dim(nodes, first, chunk, axis=1)
        near_off = lax.dynamic_slice_in_dim(offsets, first, chunk, axis=1)
    params = run_params(place, hyper_params, window, nodes, near_off, chunk)
    payload = run_chain(place, params, arrived)
    returned = [payload[0]] + [
        lax.ppermute(
            payload[shift],
            "tm",
            [(i, (i + shift) % time_count) for i in range(time_count)],
        )
        for shift in range(1, time_count)
    ]
    if chunk % 128 == 0:
        solution_out, stats_out = run_place(place, returned)
        stats_quarter = stats_out[:5]
    else:
        ordered = jnp.take(
            jnp.stack(returned),
            lax.rem(time_place - jnp.arange(time_count) + time_count, time_count),
            axis=0,
        )
        solution_out = ordered[:, :row_count].transpose(1, 0, 2).reshape(row_count, quarter)
        stats_quarter = ordered[:, row_count : row_count + 5].transpose(1, 0, 2).reshape(5, quarter)
    stats_full = lax.all_gather(stats_quarter, "hyp", axis=1, tiled=True)
    return (solution_out, stats_full[0], stats_full[1:5])


def solution(mesh):
    placed = (
        P("space"),
        P("space"),
        P("space"),
        P(None, "space"),
        P(None, "space"),
        P("tm", "space"),
        P("tm", "space"),
        P("tm", "space"),
        P("tm", "space"),
        P(),
    )
    return jax.shard_map(
        per_device_body,
        mesh=mesh,
        in_specs=placed,
        out_specs=(P("tm", ("space", "hyp")), P("space"), P(None, "space")),
        check_vma=False,
    )
```

```python
import functools

import jax
import jax.numpy as jnp
from jax import lax
from jax.experimental import pallas as pl
from jax.experimental.pallas import tpu as pltpu
from jax.sharding import PartitionSpec as P

BAND = 64
INTERPRET = False


def with_halo(block, axis, width):
    count = lax.axis_size(axis)
    if count == 2:
        place = lax.axis_index(axis)
        send = jnp.where(place == 0, block[-width:], block[:width])
        got = lax.ppermute(send, axis, [(0, 1), (1, 0)])
        low = jnp.where(place == 1, got, jnp.zeros_like(got))
        high = jnp.where(place == 0, got, jnp.zeros_like(got))
    else:
        forward = [(i, i + 1) for i in range(count - 1)]
        backward = [(target, source) for source, target in forward]
        low = lax.ppermute(block[-width:], axis, forward)
        high = lax.ppermute(block[:width], axis, backward)
    return jnp.concatenate([low, block, high])


def param_kernel(place_ref, hyper_ref, window_ref, nodes_hbm, offsets_hbm, par_ref, nodes_ref, offsets_ref, sems, *, aligned):
    width = par_ref.shape[1]
    first = pl.multiple_of(place_ref[1], 128) if aligned else 0
    node_copy = pltpu.make_async_copy(nodes_hbm.at[:, pl.ds(first, width)], nodes_ref, sems.at[0])
    offsets_copy = pltpu.make_async_copy(
        offsets_hbm.at[:, pl.ds(first, width)], offsets_ref, sems.at[1]
    )
    node_copy.start()
    offsets_copy.start()
    node_copy.wait()
    offsets_copy.wait()
    window = window_ref[...]
    span = window.shape[1]
    near_off = offsets_ref[...]
    ones = jnp.ones((1, width), jnp.float32)
    own_kappa = pltpu.roll(window, span - BAND, 1)[:, :width]
    lanes = lax.broadcasted_iota(jnp.int32, (1, width), 1)
    targets = jnp.concatenate(
        [BAND + lanes + near_off[k : k + 1, :] for k in range(near_off.shape[0])], axis=1
    )
    picks = (lax.broadcasted_iota(jnp.int32, (span, targets.shape[1]), 0) == targets).astype(
        jnp.float32
    )
    gathered = jnp.dot(
        jnp.broadcast_to(window, (8, span)),
        picks,
        precision=lax.Precision.HIGHEST,
        preferred_element_type=jnp.float32,
    )[0:1, :]
    nearby = jnp.concatenate(
        [gathered[:, k * width : (k + 1) * width] for k in range(near_off.shape[0])], axis=0
    )
    weights = nodes_ref[2:6, :]
    edge_sum = (
        weights[0:1] * nearby[0:1]
        + weights[1:2] * nearby[1:2]
        + weights[2:3] * nearby[2:3]
        + weights[3:4] * nearby[3:4]
    )
    spatial = jnp.exp(2.0 * hyper_ref[0] * ones) * (nodes_ref[0:1, :] * own_kappa + edge_sum)
    scaled = jnp.exp(hyper_ref[1] * ones) * spatial
    persist = jnp.tanh(hyper_ref[2] + nodes_ref[1:2, :])
    ns = jnp.exp(hyper_ref[3] * ones)
    ls2 = (1.0 - persist * persist) / persist
    sp = scaled * (1.0 + persist * persist)
    mps = -persist * scaled
    qs = 2.0 * persist * (1.0 - persist * persist) * scaled
    two_ls2 = 2.0 * ls2
    par_ref[0:1, :] = sp
    par_ref[1:2, :] = mps
    par_ref[2:3, :] = qs
    par_ref[3:4, :] = ns
    par_ref[4:5, :] = two_ls2
    par_ref[5:8, :] = jnp.zeros((3, width), jnp.float32)


def run_params(place, hyper, window, nodes, offsets, width):
    vmem = pl.BlockSpec(memory_space=pltpu.VMEM)
    smem = pl.BlockSpec(memory_space=pltpu.SMEM)
    hbm = pl.BlockSpec(memory_space=pl.ANY)
    return pl.pallas_call(
        functools.partial(param_kernel, aligned=nodes.shape[1] != width),
        out_shape=jax.ShapeDtypeStruct((8, width), jnp.float32),
        in_specs=[smem, smem, vmem, hbm, hbm],
        out_specs=vmem,
        scratch_shapes=[
            pltpu.VMEM((6, width), jnp.float32),
            pltpu.VMEM((4, width), jnp.int32),
            pltpu.SemaphoreType.DMA((2,)),
        ],
        interpret=INTERPRET,
    )(place, hyper, window, nodes, offsets)


def chain_kernel(*refs):
    place_ref, par_ref = refs[:2]
    blocks = (len(refs) - 7) // 2
    pieces = refs[2 : 2 + blocks]
    outs = refs[2 + blocks : 2 + 2 * blocks]
    out_ref, piv_ref, slv_ref, data_ref, piece_sems = refs[2 + 2 * blocks :]
    _, _, rows, width = data_ref.shape
    place = place_ref[0]
    piece_copies = [
        pltpu.make_async_copy(pieces[shift], data_ref.at[shift], piece_sems.at[shift])
        for shift in range(blocks)
    ]
    for copy in piece_copies:
        copy.start()
    sp = par_ref[0:1, :]
    mps = par_ref[1:2, :]
    qs = par_ref[2:3, :]
    ns = par_ref[3:4, :]
    two_ls2 = par_ref[4:5, :]
    zeros = jnp.zeros_like(sp)
    carry = (zeros,) * 11
    for copy in piece_copies:
        copy.wait()
    for block in range(blocks):
        slot = lax.rem(place - block + blocks, blocks)

        def forward(t, carry):
            inv, t0, t1, t2, t3, solved, c0, c1, c2, c3, logs = carry
            rough = data_ref[slot, 0, pl.ds(t, 1), :]
            coup = data_ref[slot, 1, pl.ds(t, 1), :]
            weight = data_ref[slot, 2, pl.ds(t, 1), :]
            obs = data_ref[slot, 3, pl.ds(t, 1), :]
            prior = sp * rough
            nugget = ns * weight
            diagonal = prior + nugget
            offdiag = mps * coup
            pivots = diagonal - offdiag * offdiag * inv
            ratios = offdiag * inv
            rr = ratios * ratios
            t0 = rr * t0 + 2.0 * prior - 4.0 * offdiag * ratios
            t1 = rr * t1 + prior - 2.0 * offdiag * ratios
            t2 = rr * t2 + qs * rough - two_ls2 * offdiag * ratios
            t3 = rr * t3 + nugget
            solved = obs - ratios * solved
            inv = 1.0 / pivots
            c0 = c0 + 0.5 * t0 * inv
            c1 = c1 + 0.5 * t1 * inv
            c2 = c2 + 0.5 * t2 * inv
            c3 = c3 + 0.5 * t3 * inv
            logs = logs + jnp.log(pivots)
            piv_ref[block, pl.ds(t, 1), :] = inv
            slv_ref[block, pl.ds(t, 1), :] = solved
            return (inv, t0, t1, t2, t3, solved, c0, c1, c2, c3, logs)

        carry = lax.fori_loop(0, rows, forward, carry, unroll=True)
    c0, c1, c2, c3, logs = carry[6:]
    closing = (zeros,) * 5
    for block in reversed(range(blocks)):
        slot = lax.rem(place - block + blocks, blocks)

        def backward(i, carry):
            t = rows - 1 - i
            following, q0, q1, q2, q3 = carry
            rough = data_ref[slot, 0, pl.ds(t, 1), :]
            coup = data_ref[slot, 1, pl.ds(t, 1), :]
            weight = data_ref[slot, 2, pl.ds(t, 1), :]
            prior = sp * rough
            nugget = ns * weight
            offdiag = mps * coup
            values = (slv_ref[block, pl.ds(t, 1), :] - following) * piv_ref[block, pl.ds(t, 1), :]
            q0 = q0 + 2.0 * prior * values * values + 4.0 * values * following
            q1 = q1 + prior * values * values + 2.0 * values * following
            q2 = q2 + qs * rough * values * values + two_ls2 * values * following
            q3 = q3 + nugget * values * values
            out_ref[block, pl.ds(t, 1), :] = values
            return (offdiag * values, q0, q1, q2, q3)

        closing = lax.fori_loop(0, rows, backward, closing, unroll=True)
    q0, q1, q2, q3 = closing[1:]
    scale = 1.0 / (rows * blocks)
    stats = jnp.concatenate(
        [
            logs * scale,
            (c0 - 0.5 * q0) * scale,
            (c1 - 0.5 * q1) * scale,
            (c2 - 0.5 * q2) * scale,
            (c3 - 0.5 * q3) * scale,
            jnp.zeros((3, width), jnp.float32),
        ],
        axis=0,
    )
    for block in range(blocks):
        out_ref[block, rows : rows + 8, :] = stats
    for shift in range(blocks):
        outs[shift][...] = out_ref[lax.rem(place + shift, blocks)]


def run_chain(place, params, pieces):
    blocks = len(pieces)
    _, rows, width = pieces[0].shape
    vmem = pl.BlockSpec(memory_space=pltpu.VMEM)
    smem = pl.BlockSpec(memory_space=pltpu.SMEM)
    hbm = pl.BlockSpec(memory_space=pl.ANY)
    return pl.pallas_call(
        chain_kernel,
        out_shape=[jax.ShapeDtypeStruct((rows + 8, width), jnp.float32)] * blocks,
        in_specs=[smem, vmem] + [hbm] * blocks,
        out_specs=[vmem] * blocks,
        scratch_shapes=[
            pltpu.VMEM((blocks, rows + 8, width), jnp.float32),
            pltpu.VMEM((blocks, rows, width), jnp.float32),
            pltpu.VMEM((blocks, rows, width), jnp.float32),
            pltpu.VMEM((blocks, 4, rows, width), jnp.float32),
            pltpu.SemaphoreType.DMA((blocks,)),
        ],
        interpret=INTERPRET,
    )(place, params, *pieces)


def place_kernel(place_ref, *refs):
    blocks = len(refs) - 2
    pieces = refs[:blocks]
    sol_ref, stat_ref = refs[blocks:]
    rows = sol_ref.shape[0]
    width = pieces[0].shape[1]
    place = place_ref[0]
    for shift in range(blocks):
        column = pl.multiple_of(lax.rem(place - shift + blocks, blocks) * width, 128)
        sol_ref[:, pl.ds(column, width)] = pieces[shift][0:rows, :]
        stat_ref[:, pl.ds(column, width)] = pieces[shift][rows : rows + 8, :]


def run_place(place, pieces):
    blocks = len(pieces)
    rows = pieces[0].shape[0] - 8
    width = pieces[0].shape[1]
    vmem = pl.BlockSpec(memory_space=pltpu.VMEM)
    smem = pl.BlockSpec(memory_space=pltpu.SMEM)
    return pl.pallas_call(
        place_kernel,
        out_shape=(
            jax.ShapeDtypeStruct((rows, blocks * width), jnp.float32),
            jax.ShapeDtypeStruct((8, blocks * width), jnp.float32),
        ),
        in_specs=[smem] + [vmem] * blocks,
        out_specs=(vmem, vmem),
        interpret=INTERPRET,
    )(place, *pieces)


def per_device_body(
    log_kappa,
    node_mass,
    rho_base,
    edge_weight,
    offsets,
    roughness,
    coupling,
    obs_weight,
    observed,
    hyper_params,
):
    row_count, full_width = roughness.shape
    time_count = lax.axis_size("tm")
    hyp_count = lax.axis_size("hyp")
    time_place = lax.axis_index("tm")
    hyp_place = lax.axis_index("hyp")
    quarter = full_width // hyp_count
    chunk = quarter // time_count
    first = hyp_place * quarter + time_place * chunk

    kappa_sq = jnp.exp(2.0 * log_kappa)
    padded = with_halo(kappa_sq, "space", BAND)

    stacked = jnp.stack([roughness, coupling, obs_weight, observed])
    pieces = [
        lax.dynamic_slice_in_dim(
            stacked,
            hyp_place * quarter + lax.rem(time_place + shift, time_count) * chunk,
            chunk,
            axis=2,
        )
        for shift in range(time_count)
    ]
    arrived = [pieces[0]] + [
        lax.ppermute(
            pieces[shift],
            "tm",
            [(i, (i + shift) % time_count) for i in range(time_count)],
        )
        for shift in range(1, time_count)
    ]
    place = jnp.stack([time_place, first]).astype(jnp.int32)
    window = lax.dynamic_slice_in_dim(padded, first, chunk + 2 * BAND)[None]
    nodes = jnp.concatenate([node_mass[None], rho_base[None], edge_weight], axis=0)
    near_off = offsets
    if chunk % 128:
        nodes = lax.dynamic_slice_in_dim(nodes, first, chunk, axis=1)
        near_off = lax.dynamic_slice_in_dim(offsets, first, chunk, axis=1)
    params = run_params(place, hyper_params, window, nodes, near_off, chunk)
    payload = run_chain(place, params, arrived)
    returned = [payload[0]] + [
        lax.ppermute(
            payload[shift],
            "tm",
            [(i, (i + shift) % time_count) for i in range(time_count)],
        )
        for shift in range(1, time_count)
    ]
    if chunk % 128 == 0:
        solution_out, stats_out = run_place(place, returned)
        stats_quarter = stats_out[:5]
    else:
        ordered = jnp.take(
            jnp.stack(returned),
            lax.rem(time_place - jnp.arange(time_count) + time_count, time_count),
            axis=0,
        )
        solution_out = ordered[:, :row_count].transpose(1, 0, 2).reshape(row_count, quarter)
        stats_quarter = ordered[:, row_count : row_count + 5].transpose(1, 0, 2).reshape(5, quarter)
    stats_full = lax.all_gather(stats_quarter, "hyp", axis=1, tiled=True)
    return (solution_out, stats_full[0], stats_full[1:5])


def solution(mesh):
    placed = (
        P("space"),
        P("space"),
        P("space"),
        P(None, "space"),
        P(None, "space"),
        P("tm", "space"),
        P("tm", "space"),
        P("tm", "space"),
        P("tm", "space"),
        P(),
    )
    return jax.shard_map(
        per_device_body,
        mesh=mesh,
        in_specs=placed,
        out_specs=(P("tm", ("space", "hyp")), P("space"), P(None, "space")),
        check_vma=False,
    )
```

```python
import functools

import jax
import jax.numpy as jnp
from jax import lax
from jax.experimental import pallas as pl
from jax.experimental.pallas import tpu as pltpu
from jax.sharding import PartitionSpec as P

BAND = 64
INTERPRET = False


def with_halo(log_block, axis, width):
    count = lax.axis_size(axis)
    low_edge = jnp.exp(2.0 * log_block[:width])
    high_edge = jnp.exp(2.0 * log_block[-width:])
    if count == 2:
        place = lax.axis_index(axis)
        send = jnp.where(place == 0, high_edge, low_edge)
        got = lax.ppermute(send, axis, [(0, 1), (1, 0)])
        low = jnp.where(place == 1, got, jnp.zeros_like(got))
        high = jnp.where(place == 0, got, jnp.zeros_like(got))
    else:
        forward = [(i, i + 1) for i in range(count - 1)]
        backward = [(target, source) for source, target in forward]
        low = lax.ppermute(high_edge, axis, forward)
        high = lax.ppermute(low_edge, axis, backward)
    return jnp.concatenate([low, jnp.exp(2.0 * log_block), high])


def chain_kernel(*refs, aligned):
    place_ref, hyper_ref, window_ref, nodes_hbm, offsets_hbm = refs[:5]
    blocks = (len(refs) - 13) // 2
    pieces = refs[5 : 5 + blocks]
    outs = refs[5 + blocks : 5 + 2 * blocks]
    out_ref, piv_ref, slv_ref, data_ref, nodes_ref, offsets_ref, sems, piece_sems = refs[5 + 2 * blocks :]
    _, _, rows, width = data_ref.shape
    first = pl.multiple_of(place_ref[1], 128) if aligned else 0
    node_copy = pltpu.make_async_copy(nodes_hbm.at[:, pl.ds(first, width)], nodes_ref, sems.at[0])
    offsets_copy = pltpu.make_async_copy(
        offsets_hbm.at[:, pl.ds(first, width)], offsets_ref, sems.at[1]
    )
    piece_copies = [
        pltpu.make_async_copy(pieces[shift], data_ref.at[shift], piece_sems.at[shift])
        for shift in range(blocks)
    ]
    node_copy.start()
    offsets_copy.start()
    for copy in piece_copies:
        copy.start()
    node_copy.wait()
    offsets_copy.wait()

    place = place_ref[0]
    window = window_ref[...]
    span = window.shape[1]
    near_off = offsets_ref[...]
    ones = jnp.ones((1, width), jnp.float32)
    nearby = jnp.zeros(near_off.shape, jnp.float32)
    own_kappa = None
    for shift in range(-BAND, BAND + 1):
        moved = pltpu.roll(window, (span - BAND - shift) % span, 1)[:, :width]
        if shift == 0:
            own_kappa = moved
        nearby = jnp.where(near_off == shift, moved, nearby)
    weights = nodes_ref[2:6, :]
    edge_sum = (
        weights[0:1] * nearby[0:1]
        + weights[1:2] * nearby[1:2]
        + weights[2:3] * nearby[2:3]
        + weights[3:4] * nearby[3:4]
    )
    spatial = jnp.exp(2.0 * hyper_ref[0] * ones) * (nodes_ref[0:1, :] * own_kappa + edge_sum)
    scaled = jnp.exp(hyper_ref[1] * ones) * spatial
    persist = jnp.tanh(hyper_ref[2] + nodes_ref[1:2, :])
    ns = jnp.exp(hyper_ref[3] * ones)
    ls2 = (1.0 - persist * persist) / persist
    sp = scaled * (1.0 + persist * persist)
    mps = -persist * scaled
    qs = 2.0 * persist * (1.0 - persist * persist) * scaled
    two_ls2 = 2.0 * ls2
    zeros = jnp.zeros_like(sp)
    carry = (zeros,) * 11
    for copy in piece_copies:
        copy.wait()
    for block in range(blocks):
        slot = lax.rem(place - block + blocks, blocks)

        def forward(t, carry):
            inv, t0, t1, t2, t3, solved, c0, c1, c2, c3, logs = carry
            rough = data_ref[slot, 0, pl.ds(t, 1), :]
            coup = data_ref[slot, 1, pl.ds(t, 1), :]
            weight = data_ref[slot, 2, pl.ds(t, 1), :]
            obs = data_ref[slot, 3, pl.ds(t, 1), :]
            prior = sp * rough
            nugget = ns * weight
            diagonal = prior + nugget
            offdiag = mps * coup
            pivots = diagonal - offdiag * offdiag * inv
            ratios = offdiag * inv
            rr = ratios * ratios
            t0 = rr * t0 + 2.0 * prior - 4.0 * offdiag * ratios
            t1 = rr * t1 + prior - 2.0 * offdiag * ratios
            t2 = rr * t2 + qs * rough - two_ls2 * offdiag * ratios
            t3 = rr * t3 + nugget
            solved = obs - ratios * solved
            inv = 1.0 / pivots
            c0 = c0 + 0.5 * t0 * inv
            c1 = c1 + 0.5 * t1 * inv
            c2 = c2 + 0.5 * t2 * inv
            c3 = c3 + 0.5 * t3 * inv
            logs = logs + jnp.log(pivots)
            piv_ref[block, pl.ds(t, 1), :] = inv
            slv_ref[block, pl.ds(t, 1), :] = solved
            return (inv, t0, t1, t2, t3, solved, c0, c1, c2, c3, logs)

        carry = lax.fori_loop(0, rows, forward, carry, unroll=True)
    c0, c1, c2, c3, logs = carry[6:]
    closing = (zeros,) * 5
    for block in reversed(range(blocks)):
        slot = lax.rem(place - block + blocks, blocks)

        def backward(i, carry):
            t = rows - 1 - i
            following, q0, q1, q2, q3 = carry
            rough = data_ref[slot, 0, pl.ds(t, 1), :]
            coup = data_ref[slot, 1, pl.ds(t, 1), :]
            weight = data_ref[slot, 2, pl.ds(t, 1), :]
            prior = sp * rough
            nugget = ns * weight
            offdiag = mps * coup
            values = (slv_ref[block, pl.ds(t, 1), :] - following) * piv_ref[block, pl.ds(t, 1), :]
            q0 = q0 + 2.0 * prior * values * values + 4.0 * values * following
            q1 = q1 + prior * values * values + 2.0 * values * following
            q2 = q2 + qs * rough * values * values + two_ls2 * values * following
            q3 = q3 + nugget * values * values
            out_ref[block, pl.ds(t, 1), :] = values
            return (offdiag * values, q0, q1, q2, q3)

        closing = lax.fori_loop(0, rows, backward, closing, unroll=True)
    q0, q1, q2, q3 = closing[1:]
    scale = 1.0 / (rows * blocks)
    stats = jnp.concatenate(
        [
            logs * scale,
            (c0 - 0.5 * q0) * scale,
            (c1 - 0.5 * q1) * scale,
            (c2 - 0.5 * q2) * scale,
            (c3 - 0.5 * q3) * scale,
            jnp.zeros((3, width), jnp.float32),
        ],
        axis=0,
    )
    for block in range(blocks):
        out_ref[block, rows : rows + 8, :] = stats
    for shift in range(blocks):
        outs[shift][...] = out_ref[lax.rem(place + shift, blocks)]


def run_chain(place, hyper, window, nodes, offsets, pieces):
    blocks = len(pieces)
    _, rows, width = pieces[0].shape
    vmem = pl.BlockSpec(memory_space=pltpu.VMEM)
    smem = pl.BlockSpec(memory_space=pltpu.SMEM)
    hbm = pl.BlockSpec(memory_space=pl.ANY)
    return pl.pallas_call(
        functools.partial(chain_kernel, aligned=nodes.shape[1] != width),
        out_shape=[jax.ShapeDtypeStruct((rows + 8, width), jnp.float32)] * blocks,
        in_specs=[smem, smem, vmem, hbm, hbm] + [hbm] * blocks,
        out_specs=[vmem] * blocks,
        scratch_shapes=[
            pltpu.VMEM((blocks, rows + 8, width), jnp.float32),
            pltpu.VMEM((blocks, rows, width), jnp.float32),
            pltpu.VMEM((blocks, rows, width), jnp.float32),
            pltpu.VMEM((blocks, 4, rows, width), jnp.float32),
            pltpu.VMEM((6, width), jnp.float32),
            pltpu.VMEM((4, width), jnp.int32),
            pltpu.SemaphoreType.DMA((2,)),
            pltpu.SemaphoreType.DMA((blocks,)),
        ],
        interpret=INTERPRET,
    )(place, hyper, window, nodes, offsets, *pieces)


def place_kernel(place_ref, *refs):
    blocks = len(refs) - 2
    pieces = refs[:blocks]
    sol_ref, stat_ref = refs[blocks:]
    rows = sol_ref.shape[0]
    width = pieces[0].shape[1]
    place = place_ref[0]
    for shift in range(blocks):
        column = pl.multiple_of(lax.rem(place - shift + blocks, blocks) * width, 128)
        sol_ref[:, pl.ds(column, width)] = pieces[shift][0:rows, :]
        stat_ref[:, pl.ds(column, width)] = pieces[shift][rows : rows + 8, :]


def run_place(place, pieces):
    blocks = len(pieces)
    rows = pieces[0].shape[0] - 8
    width = pieces[0].shape[1]
    vmem = pl.BlockSpec(memory_space=pltpu.VMEM)
    smem = pl.BlockSpec(memory_space=pltpu.SMEM)
    return pl.pallas_call(
        place_kernel,
        out_shape=(
            jax.ShapeDtypeStruct((rows, blocks * width), jnp.float32),
            jax.ShapeDtypeStruct((8, blocks * width), jnp.float32),
        ),
        in_specs=[smem] + [vmem] * blocks,
        out_specs=(vmem, vmem),
        interpret=INTERPRET,
    )(place, *pieces)


def per_device_body(
    log_kappa,
    node_mass,
    rho_base,
    edge_weight,
    offsets,
    roughness,
    coupling,
    obs_weight,
    observed,
    hyper_params,
):
    row_count, full_width = roughness.shape
    time_count = lax.axis_size("tm")
    hyp_count = lax.axis_size("hyp")
    time_place = lax.axis_index("tm")
    hyp_place = lax.axis_index("hyp")
    quarter = full_width // hyp_count
    chunk = quarter // time_count
    first = hyp_place * quarter + time_place * chunk

    padded = with_halo(log_kappa, "space", BAND)

    stacked = jnp.stack([roughness, coupling, obs_weight, observed])
    pieces = [
        lax.dynamic_slice_in_dim(
            stacked,
            hyp_place * quarter + lax.rem(time_place + shift, time_count) * chunk,
            chunk,
            axis=2,
        )
        for shift in range(time_count)
    ]
    arrived = [pieces[0]] + [
        lax.ppermute(
            pieces[shift],
            "tm",
            [(i, (i + shift) % time_count) for i in range(time_count)],
        )
        for shift in range(1, time_count)
    ]
    place = jnp.stack([time_place, first]).astype(jnp.int32)
    window = lax.dynamic_slice_in_dim(padded, first, chunk + 2 * BAND)[None]
    nodes = jnp.concatenate([node_mass[None], rho_base[None], edge_weight], axis=0)
    near_off = offsets
    if chunk % 128:
        nodes = lax.dynamic_slice_in_dim(nodes, first, chunk, axis=1)
        near_off = lax.dynamic_slice_in_dim(offsets, first, chunk, axis=1)
    payload = run_chain(place, hyper_params, window, nodes, near_off, arrived)
    returned = [payload[0]] + [
        lax.ppermute(
            payload[shift],
            "tm",
            [(i, (i + shift) % time_count) for i in range(time_count)],
        )
        for shift in range(1, time_count)
    ]
    if chunk % 128 == 0:
        solution_out, stats_out = run_place(place, returned)
        stats_quarter = stats_out[:5]
    else:
        ordered = jnp.take(
            jnp.stack(returned),
            lax.rem(time_place - jnp.arange(time_count) + time_count, time_count),
            axis=0,
        )
        solution_out = ordered[:, :row_count].transpose(1, 0, 2).reshape(row_count, quarter)
        stats_quarter = ordered[:, row_count : row_count + 5].transpose(1, 0, 2).reshape(5, quarter)
    stats_full = lax.all_gather(stats_quarter, "hyp", axis=1, tiled=True)
    return (solution_out, stats_full[0], stats_full[1:5])


def solution(mesh):
    placed = (
        P("space"),
        P("space"),
        P("space"),
        P(None, "space"),
        P(None, "space"),
        P("tm", "space"),
        P("tm", "space"),
        P("tm", "space"),
        P("tm", "space"),
        P(),
    )
    return jax.shard_map(
        per_device_body,
        mesh=mesh,
        in_specs=placed,
        out_specs=(P("tm", ("space", "hyp")), P("space"), P(None, "space")),
        check_vma=False,
    )
```

```python
import functools

import jax
import jax.numpy as jnp
from jax import lax
from jax.experimental import pallas as pl
from jax.experimental.pallas import tpu as pltpu
from jax.sharding import PartitionSpec as P

BAND = 64
INTERPRET = False


def with_halo(block, axis, width):
    count = lax.axis_size(axis)
    if count == 2:
        place = lax.axis_index(axis)
        send = jnp.where(place == 0, block[-width:], block[:width])
        got = lax.ppermute(send, axis, [(0, 1), (1, 0)])
        low = jnp.where(place == 1, got, jnp.zeros_like(got))
        high = jnp.where(place == 0, got, jnp.zeros_like(got))
    else:
        forward = [(i, i + 1) for i in range(count - 1)]
        backward = [(target, source) for source, target in forward]
        low = lax.ppermute(block[-width:], axis, forward)
        high = lax.ppermute(block[:width], axis, backward)
    return jnp.concatenate([low, block, high])


def chain_kernel(*refs, aligned):
    place_ref, hyper_ref, window_ref, nodes_hbm, offsets_hbm = refs[:5]
    blocks = (len(refs) - 13) // 2
    pieces = refs[5 : 5 + blocks]
    outs = refs[5 + blocks : 5 + 2 * blocks]
    out_ref, piv_ref, slv_ref, data_ref, nodes_ref, offsets_ref, sems, piece_sems = refs[5 + 2 * blocks :]
    _, _, rows, width = data_ref.shape
    first = pl.multiple_of(place_ref[1], 128) if aligned else 0
    node_copy = pltpu.make_async_copy(nodes_hbm.at[:, pl.ds(first, width)], nodes_ref, sems.at[0])
    offsets_copy = pltpu.make_async_copy(
        offsets_hbm.at[:, pl.ds(first, width)], offsets_ref, sems.at[1]
    )
    piece_copies = [
        pltpu.make_async_copy(pieces[shift], data_ref.at[shift], piece_sems.at[shift])
        for shift in range(blocks)
    ]
    node_copy.start()
    offsets_copy.start()
    for copy in piece_copies:
        copy.start()
    node_copy.wait()
    offsets_copy.wait()

    place = place_ref[0]
    window = window_ref[...]
    span = window.shape[1]
    near_off = offsets_ref[...]
    ones = jnp.ones((1, width), jnp.float32)
    neigh = near_off.shape[0]
    paired = jnp.concatenate(
        [
            jnp.broadcast_to(window, (neigh, span)),
            jnp.broadcast_to(pltpu.roll(window, span - 1, 1), (neigh, span)),
        ],
        axis=0,
    )
    paired_off = jnp.concatenate([near_off, near_off - 1], axis=0)
    both = jnp.zeros(paired_off.shape, jnp.float32)
    own_kappa = None
    for shift in range(-BAND, BAND + 1, 2):
        moved = pltpu.roll(paired, (span - BAND - shift) % span, 1)[:, :width]
        if shift == 0:
            own_kappa = moved[0:1]
        both = jnp.where(paired_off == shift, moved, both)
    nearby = both[:neigh] + both[neigh:]
    weights = nodes_ref[2:6, :]
    edge_sum = (
        weights[0:1] * nearby[0:1]
        + weights[1:2] * nearby[1:2]
        + weights[2:3] * nearby[2:3]
        + weights[3:4] * nearby[3:4]
    )
    spatial = jnp.exp(2.0 * hyper_ref[0] * ones) * (nodes_ref[0:1, :] * own_kappa + edge_sum)
    scaled = jnp.exp(hyper_ref[1] * ones) * spatial
    persist = jnp.tanh(hyper_ref[2] + nodes_ref[1:2, :])
    ns = jnp.exp(hyper_ref[3] * ones)
    ls2 = (1.0 - persist * persist) / persist
    sp = scaled * (1.0 + persist * persist)
    mps = -persist * scaled
    qs = 2.0 * persist * (1.0 - persist * persist) * scaled
    two_ls2 = 2.0 * ls2
    zeros = jnp.zeros_like(sp)
    carry = (zeros,) * 11
    for copy in piece_copies:
        copy.wait()
    for block in range(blocks):
        slot = lax.rem(place - block + blocks, blocks)

        def forward(t, carry):
            inv, t0, t1, t2, t3, solved, c0, c1, c2, c3, logs = carry
            rough = data_ref[slot, 0, pl.ds(t, 1), :]
            coup = data_ref[slot, 1, pl.ds(t, 1), :]
            weight = data_ref[slot, 2, pl.ds(t, 1), :]
            obs = data_ref[slot, 3, pl.ds(t, 1), :]
            prior = sp * rough
            nugget = ns * weight
            diagonal = prior + nugget
            offdiag = mps * coup
            pivots = diagonal - offdiag * offdiag * inv
            ratios = offdiag * inv
            rr = ratios * ratios
            od_r = offdiag * ratios
            t0 = rr * t0 + 2.0 * prior - 4.0 * od_r
            t1 = rr * t1 + prior - 2.0 * od_r
            t2 = rr * t2 + qs * rough - two_ls2 * offdiag * ratios
            t3 = rr * t3 + nugget
            solved = obs - ratios * solved
            inv = 1.0 / pivots
            half_inv = 0.5 * inv
            c0 = c0 + t0 * half_inv
            c1 = c1 + t1 * half_inv
            c2 = c2 + t2 * half_inv
            c3 = c3 + t3 * half_inv
            logs = logs + jnp.log(pivots)
            piv_ref[block, pl.ds(t, 1), :] = inv
            slv_ref[block, pl.ds(t, 1), :] = solved
            return (inv, t0, t1, t2, t3, solved, c0, c1, c2, c3, logs)

        carry = lax.fori_loop(0, rows, forward, carry, unroll=True)
    c0, c1, c2, c3, logs = carry[6:]
    closing = (zeros,) * 5
    for block in reversed(range(blocks)):
        slot = lax.rem(place - block + blocks, blocks)

        def backward(i, carry):
            t = rows - 1 - i
            following, q0, q1, q2, q3 = carry
            rough = data_ref[slot, 0, pl.ds(t, 1), :]
            coup = data_ref[slot, 1, pl.ds(t, 1), :]
            weight = data_ref[slot, 2, pl.ds(t, 1), :]
            prior = sp * rough
            nugget = ns * weight
            offdiag = mps * coup
            values = (slv_ref[block, pl.ds(t, 1), :] - following) * piv_ref[block, pl.ds(t, 1), :]
            pvv = prior * values * values
            vf = values * following
            q0 = q0 + 2.0 * pvv + 4.0 * vf
            q1 = q1 + pvv + 2.0 * vf
            q2 = q2 + qs * rough * values * values + two_ls2 * values * following
            q3 = q3 + nugget * values * values
            out_ref[block, pl.ds(t, 1), :] = values
            return (offdiag * values, q0, q1, q2, q3)

        closing = lax.fori_loop(0, rows, backward, closing, unroll=True)
    q0, q1, q2, q3 = closing[1:]
    scale = 1.0 / (rows * blocks)
    stats = jnp.concatenate(
        [
            logs * scale,
            (c0 - 0.5 * q0) * scale,
            (c1 - 0.5 * q1) * scale,
            (c2 - 0.5 * q2) * scale,
            (c3 - 0.5 * q3) * scale,
            jnp.zeros((3, width), jnp.float32),
        ],
        axis=0,
    )
    for block in range(blocks):
        out_ref[block, rows : rows + 8, :] = stats
    for shift in range(blocks):
        outs[shift][...] = out_ref[lax.rem(place + shift, blocks)]


def run_chain(place, hyper, window, nodes, offsets, pieces):
    blocks = len(pieces)
    _, rows, width = pieces[0].shape
    vmem = pl.BlockSpec(memory_space=pltpu.VMEM)
    smem = pl.BlockSpec(memory_space=pltpu.SMEM)
    hbm = pl.BlockSpec(memory_space=pl.ANY)
    return pl.pallas_call(
        functools.partial(chain_kernel, aligned=nodes.shape[1] != width),
        out_shape=[jax.ShapeDtypeStruct((rows + 8, width), jnp.float32)] * blocks,
        in_specs=[smem, smem, vmem, hbm, hbm] + [hbm] * blocks,
        out_specs=[vmem] * blocks,
        scratch_shapes=[
            pltpu.VMEM((blocks, rows + 8, width), jnp.float32),
            pltpu.VMEM((blocks, rows, width), jnp.float32),
            pltpu.VMEM((blocks, rows, width), jnp.float32),
            pltpu.VMEM((blocks, 4, rows, width), jnp.float32),
            pltpu.VMEM((6, width), jnp.float32),
            pltpu.VMEM((4, width), jnp.int32),
            pltpu.SemaphoreType.DMA((2,)),
            pltpu.SemaphoreType.DMA((blocks,)),
        ],
        interpret=INTERPRET,
    )(place, hyper, window, nodes, offsets, *pieces)


def place_kernel(place_ref, *refs):
    blocks = len(refs) - 2
    pieces = refs[:blocks]
    sol_ref, stat_ref = refs[blocks:]
    rows = sol_ref.shape[0]
    width = pieces[0].shape[1]
    place = place_ref[0]
    for shift in range(blocks):
        column = pl.multiple_of(lax.rem(place - shift + blocks, blocks) * width, 128)
        sol_ref[:, pl.ds(column, width)] = pieces[shift][0:rows, :]
        stat_ref[:, pl.ds(column, width)] = pieces[shift][rows : rows + 8, :]


def run_place(place, pieces):
    blocks = len(pieces)
    rows = pieces[0].shape[0] - 8
    width = pieces[0].shape[1]
    vmem = pl.BlockSpec(memory_space=pltpu.VMEM)
    smem = pl.BlockSpec(memory_space=pltpu.SMEM)
    return pl.pallas_call(
        place_kernel,
        out_shape=(
            jax.ShapeDtypeStruct((rows, blocks * width), jnp.float32),
            jax.ShapeDtypeStruct((8, blocks * width), jnp.float32),
        ),
        in_specs=[smem] + [vmem] * blocks,
        out_specs=(vmem, vmem),
        interpret=INTERPRET,
    )(place, *pieces)


def per_device_body(
    log_kappa,
    node_mass,
    rho_base,
    edge_weight,
    offsets,
    roughness,
    coupling,
    obs_weight,
    observed,
    hyper_params,
):
    row_count, full_width = roughness.shape
    time_count = lax.axis_size("tm")
    hyp_count = lax.axis_size("hyp")
    time_place = lax.axis_index("tm")
    hyp_place = lax.axis_index("hyp")
    quarter = full_width // hyp_count
    chunk = quarter // time_count
    first = hyp_place * quarter + time_place * chunk

    kappa_sq = jnp.exp(2.0 * log_kappa)
    padded = with_halo(kappa_sq, "space", BAND)

    stacked = jnp.stack([roughness, coupling, obs_weight, observed])
    pieces = [
        lax.dynamic_slice_in_dim(
            stacked,
            hyp_place * quarter + lax.rem(time_place + shift, time_count) * chunk,
            chunk,
            axis=2,
        )
        for shift in range(time_count)
    ]
    arrived = [pieces[0]] + [
        lax.ppermute(
            pieces[shift],
            "tm",
            [(i, (i + shift) % time_count) for i in range(time_count)],
        )
        for shift in range(1, time_count)
    ]
    place = jnp.stack([time_place, first]).astype(jnp.int32)
    window = lax.dynamic_slice_in_dim(padded, first, chunk + 2 * BAND)[None]
    nodes = jnp.concatenate([node_mass[None], rho_base[None], edge_weight], axis=0)
    near_off = offsets
    if chunk % 128:
        nodes = lax.dynamic_slice_in_dim(nodes, first, chunk, axis=1)
        near_off = lax.dynamic_slice_in_dim(offsets, first, chunk, axis=1)
    payload = run_chain(place, hyper_params, window, nodes, near_off, arrived)
    returned = [payload[0]] + [
        lax.ppermute(
            payload[shift],
            "tm",
            [(i, (i + shift) % time_count) for i in range(time_count)],
        )
        for shift in range(1, time_count)
    ]
    if chunk % 128 == 0:
        solution_out, stats_out = run_place(place, returned)
        stats_quarter = stats_out[:5]
    else:
        ordered = jnp.take(
            jnp.stack(returned),
            lax.rem(time_place - jnp.arange(time_count) + time_count, time_count),
            axis=0,
        )
        solution_out = ordered[:, :row_count].transpose(1, 0, 2).reshape(row_count, quarter)
        stats_quarter = ordered[:, row_count : row_count + 5].transpose(1, 0, 2).reshape(5, quarter)
    stats_full = lax.all_gather(stats_quarter, "hyp", axis=1, tiled=True)
    return (solution_out, stats_full[0], stats_full[1:5])


def solution(mesh):
    placed = (
        P("space"),
        P("space"),
        P("space"),
        P(None, "space"),
        P(None, "space"),
        P("tm", "space"),
        P("tm", "space"),
        P("tm", "space"),
        P("tm", "space"),
        P(),
    )
    return jax.shard_map(
        per_device_body,
        mesh=mesh,
        in_specs=placed,
        out_specs=(P("tm", ("space", "hyp")), P("space"), P(None, "space")),
        check_vma=False,
    )
```

```python
import functools

import jax
import jax.numpy as jnp
from jax import lax
from jax.experimental import pallas as pl
from jax.experimental.pallas import tpu as pltpu
from jax.sharding import PartitionSpec as P

BAND = 64
INTERPRET = False


def with_halo(block, axis, width):
    count = lax.axis_size(axis)
    if count == 2:
        place = lax.axis_index(axis)
        send = jnp.where(place == 0, block[-width:], block[:width])
        got = lax.ppermute(send, axis, [(0, 1), (1, 0)])
        low = jnp.where(place == 1, got, jnp.zeros_like(got))
        high = jnp.where(place == 0, got, jnp.zeros_like(got))
    else:
        forward = [(i, i + 1) for i in range(count - 1)]
        backward = [(target, source) for source, target in forward]
        low = lax.ppermute(block[-width:], axis, forward)
        high = lax.ppermute(block[:width], axis, backward)
    return jnp.concatenate([low, block, high])


def chain_kernel(*refs, aligned):
    place_ref, hyper_ref, window_ref, nodes_hbm, offsets_hbm = refs[:5]
    blocks = (len(refs) - 13) // 2
    pieces = refs[5 : 5 + blocks]
    outs = refs[5 + blocks : 5 + 2 * blocks]
    out_ref, piv_ref, slv_ref, data_ref, nodes_ref, offsets_ref, sems, piece_sems = refs[5 + 2 * blocks :]
    _, _, rows, width = data_ref.shape
    first = pl.multiple_of(place_ref[1], 128) if aligned else 0
    node_copy = pltpu.make_async_copy(nodes_hbm.at[:, pl.ds(first, width)], nodes_ref, sems.at[0])
    offsets_copy = pltpu.make_async_copy(
        offsets_hbm.at[:, pl.ds(first, width)], offsets_ref, sems.at[1]
    )
    piece_copies = [
        pltpu.make_async_copy(pieces[shift], data_ref.at[shift], piece_sems.at[shift])
        for shift in range(blocks)
    ]
    node_copy.start()
    offsets_copy.start()
    for copy in piece_copies:
        copy.start()
    node_copy.wait()
    offsets_copy.wait()

    place = place_ref[0]
    window = window_ref[...]
    span = window.shape[1]
    near_off = offsets_ref[...]
    ones = jnp.ones((1, width), jnp.float32)
    neigh = near_off.shape[0]
    paired = jnp.concatenate(
        [
            jnp.broadcast_to(window, (neigh, span)),
            jnp.broadcast_to(pltpu.roll(window, span - 1, 1), (neigh, span)),
        ],
        axis=0,
    )
    paired_off = jnp.concatenate([near_off, near_off - 1], axis=0)
    both = jnp.zeros(paired_off.shape, jnp.float32)
    own_kappa = None
    for shift in range(-BAND, BAND + 1, 2):
        moved = pltpu.roll(paired, (span - BAND - shift) % span, 1)[:, :width]
        if shift == 0:
            own_kappa = moved[0:1]
        both = jnp.where(paired_off == shift, moved, both)
    nearby = both[:neigh] + both[neigh:]
    weights = nodes_ref[2:6, :]
    edge_sum = (
        weights[0:1] * nearby[0:1]
        + weights[1:2] * nearby[1:2]
        + weights[2:3] * nearby[2:3]
        + weights[3:4] * nearby[3:4]
    )
    spatial = jnp.exp(2.0 * hyper_ref[0] * ones) * (nodes_ref[0:1, :] * own_kappa + edge_sum)
    scaled = jnp.exp(hyper_ref[1] * ones) * spatial
    persist = jnp.tanh(hyper_ref[2] + nodes_ref[1:2, :])
    ns = jnp.exp(hyper_ref[3] * ones)
    ls2 = (1.0 - persist * persist) / persist
    sp = scaled * (1.0 + persist * persist)
    mps = -persist * scaled
    qs = 2.0 * persist * (1.0 - persist * persist) * scaled
    two_ls2 = 2.0 * ls2
    zeros = jnp.zeros_like(sp)
    carry = (zeros,) * 11
    for copy in piece_copies:
        copy.wait()
    for block in range(blocks):
        slot = lax.rem(place - block + blocks, blocks)

        def forward(t, carry):
            inv, t0, t1, t2, t3, solved, c0, c1, c2, c3, logs = carry
            rough = data_ref[slot, 0, pl.ds(t, 1), :]
            coup = data_ref[slot, 1, pl.ds(t, 1), :]
            weight = data_ref[slot, 2, pl.ds(t, 1), :]
            obs = data_ref[slot, 3, pl.ds(t, 1), :]
            prior = sp * rough
            nugget = ns * weight
            diagonal = prior + nugget
            offdiag = mps * coup
            pivots = diagonal - offdiag * offdiag * inv
            ratios = offdiag * inv
            rr = ratios * ratios
            t0 = rr * t0 + 2.0 * prior - 4.0 * offdiag * ratios
            t1 = rr * t1 + prior - 2.0 * offdiag * ratios
            t2 = rr * t2 + qs * rough - two_ls2 * offdiag * ratios
            t3 = rr * t3 + nugget
            solved = obs - ratios * solved
            inv = 1.0 / pivots
            c0 = c0 + 0.5 * t0 * inv
            c1 = c1 + 0.5 * t1 * inv
            c2 = c2 + 0.5 * t2 * inv
            c3 = c3 + 0.5 * t3 * inv
            logs = logs + jnp.log(pivots)
            piv_ref[block, pl.ds(t, 1), :] = inv
            slv_ref[block, pl.ds(t, 1), :] = solved
            return (inv, t0, t1, t2, t3, solved, c0, c1, c2, c3, logs)

        carry = lax.fori_loop(0, rows, forward, carry, unroll=True)
    c0, c1, c2, c3, logs = carry[6:]
    closing = (zeros,) * 5
    for block in reversed(range(blocks)):
        slot = lax.rem(place - block + blocks, blocks)

        def backward(i, carry):
            t = rows - 1 - i
            following, q0, q1, q2, q3 = carry
            rough = data_ref[slot, 0, pl.ds(t, 1), :]
            coup = data_ref[slot, 1, pl.ds(t, 1), :]
            weight = data_ref[slot, 2, pl.ds(t, 1), :]
            prior = sp * rough
            nugget = ns * weight
            offdiag = mps * coup
            values = (slv_ref[block, pl.ds(t, 1), :] - following) * piv_ref[block, pl.ds(t, 1), :]
            q0 = q0 + 2.0 * prior * values * values + 4.0 * values * following
            q1 = q1 + prior * values * values + 2.0 * values * following
            q2 = q2 + qs * rough * values * values + two_ls2 * values * following
            q3 = q3 + nugget * values * values
            out_ref[block, pl.ds(t, 1), :] = values
            return (offdiag * values, q0, q1, q2, q3)

        closing = lax.fori_loop(0, rows, backward, closing, unroll=True)
    q0, q1, q2, q3 = closing[1:]
    scale = 1.0 / (rows * blocks)
    stats = jnp.concatenate(
        [
            logs * scale,
            (c0 - 0.5 * q0) * scale,
            (c1 - 0.5 * q1) * scale,
            (c2 - 0.5 * q2) * scale,
            (c3 - 0.5 * q3) * scale,
            jnp.zeros((3, width), jnp.float32),
        ],
        axis=0,
    )
    for block in range(blocks):
        out_ref[block, rows : rows + 8, :] = stats
    for shift in range(blocks):
        outs[shift][...] = out_ref[lax.rem(place + shift, blocks)]


def run_chain(place, hyper, window, nodes, offsets, pieces):
    blocks = len(pieces)
    _, rows, width = pieces[0].shape
    vmem = pl.BlockSpec(memory_space=pltpu.VMEM)
    smem = pl.BlockSpec(memory_space=pltpu.SMEM)
    hbm = pl.BlockSpec(memory_space=pl.ANY)
    return pl.pallas_call(
        functools.partial(chain_kernel, aligned=nodes.shape[1] != width),
        out_shape=[jax.ShapeDtypeStruct((rows + 8, width), jnp.float32)] * blocks,
        in_specs=[smem, smem, vmem, hbm, hbm] + [hbm] * blocks,
        out_specs=[vmem] * blocks,
        scratch_shapes=[
            pltpu.VMEM((blocks, rows + 8, width), jnp.float32),
            pltpu.VMEM((blocks, rows, width), jnp.float32),
            pltpu.VMEM((blocks, rows, width), jnp.float32),
            pltpu.VMEM((blocks, 4, rows, width), jnp.float32),
            pltpu.VMEM((6, width), jnp.float32),
            pltpu.VMEM((4, width), jnp.int32),
            pltpu.SemaphoreType.DMA((2,)),
            pltpu.SemaphoreType.DMA((blocks,)),
        ],
        interpret=INTERPRET,
    )(place, hyper, window, nodes, offsets, *pieces)


def place_kernel(place_ref, *refs):
    blocks = len(refs) - 2
    pieces = refs[:blocks]
    sol_ref, stat_ref = refs[blocks:]
    rows = sol_ref.shape[0]
    width = pieces[0].shape[1]
    place = place_ref[0]
    for shift in range(blocks):
        column = pl.multiple_of(lax.rem(place - shift + blocks, blocks) * width, 128)
        sol_ref[:, pl.ds(column, width)] = pieces[shift][0:rows, :]
        stat_ref[:, pl.ds(column, width)] = pieces[shift][rows : rows + 8, :]


def run_place(place, pieces):
    blocks = len(pieces)
    rows = pieces[0].shape[0] - 8
    width = pieces[0].shape[1]
    vmem = pl.BlockSpec(memory_space=pltpu.VMEM)
    smem = pl.BlockSpec(memory_space=pltpu.SMEM)
    return pl.pallas_call(
        place_kernel,
        out_shape=(
            jax.ShapeDtypeStruct((rows, blocks * width), jnp.float32),
            jax.ShapeDtypeStruct((8, blocks * width), jnp.float32),
        ),
        in_specs=[smem] + [vmem] * blocks,
        out_specs=(vmem, vmem),
        interpret=INTERPRET,
    )(place, *pieces)


def per_device_body(
    log_kappa,
    node_mass,
    rho_base,
    edge_weight,
    offsets,
    roughness,
    coupling,
    obs_weight,
    observed,
    hyper_params,
):
    row_count, full_width = roughness.shape
    time_count = lax.axis_size("tm")
    hyp_count = lax.axis_size("hyp")
    time_place = lax.axis_index("tm")
    hyp_place = lax.axis_index("hyp")
    quarter = full_width // hyp_count
    chunk = quarter // time_count
    first = hyp_place * quarter + time_place * chunk

    kappa_sq = jnp.exp(2.0 * log_kappa)
    padded = with_halo(kappa_sq, "space", BAND)

    stacked = jnp.stack([roughness, coupling, obs_weight, observed])
    pieces = [
        lax.dynamic_slice_in_dim(
            stacked,
            hyp_place * quarter + lax.rem(time_place + shift, time_count) * chunk,
            chunk,
            axis=2,
        )
        for shift in range(time_count)
    ]
    arrived = [pieces[0]] + [
        lax.ppermute(
            pieces[shift],
            "tm",
            [(i, (i + shift) % time_count) for i in range(time_count)],
        )
        for shift in range(1, time_count)
    ]
    place = jnp.stack([time_place, first]).astype(jnp.int32)
    window = lax.dynamic_slice_in_dim(padded, first, chunk + 2 * BAND)[None]
    nodes = jnp.concatenate([node_mass[None], rho_base[None], edge_weight], axis=0)
    near_off = offsets
    if chunk % 128:
        nodes = lax.dynamic_slice_in_dim(nodes, first, chunk, axis=1)
        near_off = lax.dynamic_slice_in_dim(offsets, first, chunk, axis=1)
    payload = run_chain(place, hyper_params, window, nodes, near_off, arrived)
    returned = [payload[0]] + [
        lax.ppermute(
            payload[shift],
            "tm",
            [(i, (i + shift) % time_count) for i in range(time_count)],
        )
        for shift in range(1, time_count)
    ]
    if chunk % 128 == 0:
        solution_out, stats_out = run_place(place, returned)
        stats_quarter = stats_out[:5]
    else:
        ordered = jnp.take(
            jnp.stack(returned),
            lax.rem(time_place - jnp.arange(time_count) + time_count, time_count),
            axis=0,
        )
        solution_out = ordered[:, :row_count].transpose(1, 0, 2).reshape(row_count, quarter)
        stats_quarter = ordered[:, row_count : row_count + 5].transpose(1, 0, 2).reshape(5, quarter)
    stats_full = lax.all_gather(stats_quarter, "hyp", axis=1, tiled=True)
    return (solution_out, stats_full[0], stats_full[1:5])


def solution(mesh):
    placed = (
        P("space"),
        P("space"),
        P("space"),
        P(None, "space"),
        P(None, "space"),
        P("tm", "space"),
        P("tm", "space"),
        P("tm", "space"),
        P("tm", "space"),
        P(),
    )
    return jax.shard_map(
        per_device_body,
        mesh=mesh,
        in_specs=placed,
        out_specs=(P("tm", ("space", "hyp")), P("space"), P(None, "space")),
        check_vma=False,
    )
```

```python
import functools

import jax
import jax.numpy as jnp
from jax import lax
from jax.experimental import pallas as pl
from jax.experimental.pallas import tpu as pltpu
from jax.sharding import PartitionSpec as P

BAND = 64
INTERPRET = False


def with_halo(block, axis, width):
    count = lax.axis_size(axis)
    if count == 2:
        place = lax.axis_index(axis)
        send = jnp.where(place == 0, block[-width:], block[:width])
        got = lax.ppermute(send, axis, [(0, 1), (1, 0)])
        low = jnp.where(place == 1, got, jnp.zeros_like(got))
        high = jnp.where(place == 0, got, jnp.zeros_like(got))
    else:
        forward = [(i, i + 1) for i in range(count - 1)]
        backward = [(target, source) for source, target in forward]
        low = lax.ppermute(block[-width:], axis, forward)
        high = lax.ppermute(block[:width], axis, backward)
    return jnp.concatenate([low, block, high])


def chain_kernel(*refs, aligned):
    place_ref, hyper_ref, window_ref, nodes_hbm, offsets_hbm = refs[:5]
    blocks = (len(refs) - 13) // 2
    pieces = refs[5 : 5 + blocks]
    outs = refs[5 + blocks : 5 + 2 * blocks]
    out_ref, piv_ref, slv_ref, data_ref, nodes_ref, offsets_ref, sems, piece_sems = refs[5 + 2 * blocks :]
    _, _, rows, width = data_ref.shape
    first = pl.multiple_of(place_ref[1], 128) if aligned else 0
    node_copy = pltpu.make_async_copy(nodes_hbm.at[:, pl.ds(first, width)], nodes_ref, sems.at[0])
    offsets_copy = pltpu.make_async_copy(
        offsets_hbm.at[:, pl.ds(first, width)], offsets_ref, sems.at[1]
    )
    piece_copies = [
        pltpu.make_async_copy(pieces[shift], data_ref.at[shift], piece_sems.at[shift])
        for shift in range(blocks)
    ]
    node_copy.start()
    offsets_copy.start()
    for copy in piece_copies:
        copy.start()
    node_copy.wait()
    offsets_copy.wait()

    place = place_ref[0]
    window = window_ref[...]
    span = window.shape[1]
    near_off = offsets_ref[...]
    ones = jnp.ones((1, width), jnp.float32)
    neigh = near_off.shape[0]
    paired = jnp.concatenate(
        [
            jnp.broadcast_to(window, (neigh, span)),
            jnp.broadcast_to(pltpu.roll(window, span - 1, 1), (neigh, span)),
        ],
        axis=0,
    )
    paired_off = jnp.concatenate([near_off, near_off - 1], axis=0)
    both = jnp.zeros(paired_off.shape, jnp.float32)
    own_kappa = None
    for shift in range(-BAND, BAND + 1, 2):
        moved = pltpu.roll(paired, (span - BAND - shift) % span, 1)[:, :width]
        if shift == 0:
            own_kappa = moved[0:1]
        both = jnp.where(paired_off == shift, moved, both)
    nearby = both[:neigh] + both[neigh:]
    weights = nodes_ref[2:6, :]
    edge_sum = (
        weights[0:1] * nearby[0:1]
        + weights[1:2] * nearby[1:2]
        + weights[2:3] * nearby[2:3]
        + weights[3:4] * nearby[3:4]
    )
    spatial = jnp.exp(2.0 * hyper_ref[0] * ones) * (nodes_ref[0:1, :] * own_kappa + edge_sum)
    scaled = jnp.exp(hyper_ref[1] * ones) * spatial
    persist = jnp.tanh(hyper_ref[2] + nodes_ref[1:2, :])
    ns = jnp.exp(hyper_ref[3] * ones)
    ls2 = (1.0 - persist * persist) / persist
    sp = scaled * (1.0 + persist * persist)
    mps = -persist * scaled
    qs = 2.0 * persist * (1.0 - persist * persist) * scaled
    two_ls2 = 2.0 * ls2
    zeros = jnp.zeros_like(sp)
    carry = (zeros,) * 11
    for copy in piece_copies:
        copy.wait()
    for block in range(blocks):
        slot = lax.rem(place - block + blocks, blocks)

        def forward(t, carry):
            inv, t0, t1, t2, t3, solved, c0, c1, c2, c3, logs = carry
            rough = data_ref[slot, 0, pl.ds(t, 1), :]
            coup = data_ref[slot, 1, pl.ds(t, 1), :]
            weight = data_ref[slot, 2, pl.ds(t, 1), :]
            obs = data_ref[slot, 3, pl.ds(t, 1), :]
            prior = sp * rough
            nugget = ns * weight
            diagonal = prior + nugget
            offdiag = mps * coup
            pivots = diagonal - offdiag * offdiag * inv
            ratios = offdiag * inv
            rr = ratios * ratios
            t0 = rr * t0 + 2.0 * prior - 4.0 * offdiag * ratios
            t1 = rr * t1 + prior - 2.0 * offdiag * ratios
            t2 = rr * t2 + qs * rough - two_ls2 * offdiag * ratios
            t3 = rr * t3 + nugget
            solved = obs - ratios * solved
            inv = 1.0 / pivots
            c0 = c0 + 0.5 * t0 * inv
            c1 = c1 + 0.5 * t1 * inv
            c2 = c2 + 0.5 * t2 * inv
            c3 = c3 + 0.5 * t3 * inv
            logs = logs + jnp.log(pivots)
            piv_ref[block, pl.ds(t, 1), :] = inv
            slv_ref[block, pl.ds(t, 1), :] = solved
            return (inv, t0, t1, t2, t3, solved, c0, c1, c2, c3, logs)

        carry = lax.fori_loop(0, rows, forward, carry, unroll=True)
    c0, c1, c2, c3, logs = carry[6:]
    closing = (zeros,) * 5
    for block in reversed(range(blocks)):
        slot = lax.rem(place - block + blocks, blocks)

        def backward(i, carry):
            t = rows - 1 - i
            following, q0, q1, q2, q3 = carry
            rough = data_ref[slot, 0, pl.ds(t, 1), :]
            coup = data_ref[slot, 1, pl.ds(t, 1), :]
            weight = data_ref[slot, 2, pl.ds(t, 1), :]
            prior = sp * rough
            nugget = ns * weight
            offdiag = mps * coup
            values = (slv_ref[block, pl.ds(t, 1), :] - following) * piv_ref[block, pl.ds(t, 1), :]
            q0 = q0 + 2.0 * prior * values * values + 4.0 * values * following
            q1 = q1 + prior * values * values + 2.0 * values * following
            q2 = q2 + qs * rough * values * values + two_ls2 * values * following
            q3 = q3 + nugget * values * values
            out_ref[block, pl.ds(t, 1), :] = values
            return (offdiag * values, q0, q1, q2, q3)

        closing = lax.fori_loop(0, rows, backward, closing, unroll=True)
    q0, q1, q2, q3 = closing[1:]
    scale = 1.0 / (rows * blocks)
    stats = jnp.concatenate(
        [
            logs * scale,
            (c0 - 0.5 * q0) * scale,
            (c1 - 0.5 * q1) * scale,
            (c2 - 0.5 * q2) * scale,
            (c3 - 0.5 * q3) * scale,
            jnp.zeros((3, width), jnp.float32),
        ],
        axis=0,
    )
    for block in range(blocks):
        out_ref[block, rows : rows + 8, :] = stats
    for shift in range(blocks):
        outs[shift][...] = out_ref[lax.rem(place + shift, blocks)]


def run_chain(place, hyper, window, nodes, offsets, pieces):
    blocks = len(pieces)
    _, rows, width = pieces[0].shape
    vmem = pl.BlockSpec(memory_space=pltpu.VMEM)
    smem = pl.BlockSpec(memory_space=pltpu.SMEM)
    hbm = pl.BlockSpec(memory_space=pl.ANY)
    return pl.pallas_call(
        functools.partial(chain_kernel, aligned=nodes.shape[1] != width),
        out_shape=[jax.ShapeDtypeStruct((rows + 8, width), jnp.float32)] * blocks,
        in_specs=[smem, smem, vmem, hbm, hbm] + [hbm] * blocks,
        out_specs=[vmem] * blocks,
        scratch_shapes=[
            pltpu.VMEM((blocks, rows + 8, width), jnp.float32),
            pltpu.VMEM((blocks, rows, width), jnp.float32),
            pltpu.VMEM((blocks, rows, width), jnp.float32),
            pltpu.VMEM((blocks, 4, rows, width), jnp.float32),
            pltpu.VMEM((6, width), jnp.float32),
            pltpu.VMEM((4, width), jnp.int32),
            pltpu.SemaphoreType.DMA((2,)),
            pltpu.SemaphoreType.DMA((blocks,)),
        ],
        interpret=INTERPRET,
    )(place, hyper, window, nodes, offsets, *pieces)


def place_kernel(place_ref, *refs):
    blocks = len(refs) - 2
    pieces = refs[:blocks]
    sol_ref, stat_ref = refs[blocks:]
    rows = sol_ref.shape[0]
    width = pieces[0].shape[1]
    place = place_ref[0]
    for shift in range(blocks):
        column = pl.multiple_of(lax.rem(place - shift + blocks, blocks) * width, 128)
        sol_ref[:, pl.ds(column, width)] = pieces[shift][0:rows, :]
        stat_ref[:, pl.ds(column, width)] = pieces[shift][rows : rows + 8, :]


def run_place(place, pieces):
    blocks = len(pieces)
    rows = pieces[0].shape[0] - 8
    width = pieces[0].shape[1]
    vmem = pl.BlockSpec(memory_space=pltpu.VMEM)
    smem = pl.BlockSpec(memory_space=pltpu.SMEM)
    return pl.pallas_call(
        place_kernel,
        out_shape=(
            jax.ShapeDtypeStruct((rows, blocks * width), jnp.float32),
            jax.ShapeDtypeStruct((8, blocks * width), jnp.float32),
        ),
        in_specs=[smem] + [vmem] * blocks,
        out_specs=(vmem, vmem),
        interpret=INTERPRET,
    )(place, *pieces)


def per_device_body(
    log_kappa,
    node_mass,
    rho_base,
    edge_weight,
    offsets,
    roughness,
    coupling,
    obs_weight,
    observed,
    hyper_params,
):
    row_count, full_width = roughness.shape
    time_count = lax.axis_size("tm")
    hyp_count = lax.axis_size("hyp")
    time_place = lax.axis_index("tm")
    hyp_place = lax.axis_index("hyp")
    quarter = full_width // hyp_count
    chunk = quarter // time_count
    first = hyp_place * quarter + time_place * chunk

    kappa_sq = jnp.exp(2.0 * log_kappa)
    padded = with_halo(kappa_sq, "space", BAND)

    stacked = jnp.stack([roughness, coupling, obs_weight, observed])
    pieces = [
        lax.dynamic_slice_in_dim(
            stacked,
            hyp_place * quarter + lax.rem(time_place + shift, time_count) * chunk,
            chunk,
            axis=2,
        )
        for shift in range(time_count)
    ]
    arrived = [pieces[0]]
    for shift in range(1, time_count):
        arrived.append(
            lax.ppermute(
                pieces[shift],
                "tm",
                [(i, (i + shift) % time_count) for i in range(time_count)],
            )
        )
    place = jnp.stack([time_place, first]).astype(jnp.int32)
    window = lax.dynamic_slice_in_dim(padded, first, chunk + 2 * BAND)[None]
    nodes = jnp.concatenate([node_mass[None], rho_base[None], edge_weight], axis=0)
    near_off = offsets
    if chunk % 128:
        nodes = lax.dynamic_slice_in_dim(nodes, first, chunk, axis=1)
        near_off = lax.dynamic_slice_in_dim(offsets, first, chunk, axis=1)
    payload = run_chain(place, hyper_params, window, nodes, near_off, arrived)
    returned = [payload[0]] + [
        lax.ppermute(
            payload[shift],
            "tm",
            [(i, (i + shift) % time_count) for i in range(time_count)],
        )
        for shift in range(1, time_count)
    ]
    if chunk % 128 == 0:
        solution_out, stats_out = run_place(place, returned)
        stats_quarter = stats_out[:5]
    else:
        ordered = jnp.take(
            jnp.stack(returned),
            lax.rem(time_place - jnp.arange(time_count) + time_count, time_count),
            axis=0,
        )
        solution_out = ordered[:, :row_count].transpose(1, 0, 2).reshape(row_count, quarter)
        stats_quarter = ordered[:, row_count : row_count + 5].transpose(1, 0, 2).reshape(5, quarter)
    stats_full = lax.all_gather(stats_quarter, "hyp", axis=1, tiled=True)
    return (solution_out, stats_full[0], stats_full[1:5])


def solution(mesh):
    placed = (
        P("space"),
        P("space"),
        P("space"),
        P(None, "space"),
        P(None, "space"),
        P("tm", "space"),
        P("tm", "space"),
        P("tm", "space"),
        P("tm", "space"),
        P(),
    )
    return jax.shard_map(
        per_device_body,
        mesh=mesh,
        in_specs=placed,
        out_specs=(P("tm", ("space", "hyp")), P("space"), P(None, "space")),
        check_vma=False,
    )
```
